32 devices in a mesh: tm: 8 (over z, y), rows: 4 (over x, core).
Axes of the slice: x: 2, y: 2, z: 4, core: 2. Of those that a mesh axis runs over, the one named last changes fastest.
Arguments:
- pivot_blocks: float32 [8, 512, 512], P('tm'), may hold values from -4 to 24, as said below
- lower_blocks: float32 [8, 512, 512], P('tm', None, 'rows'), may hold values from -5 to 0.5
- top_diagonal: float32 [8, 512, 512], P('tm', 'rows'), may hold values from -1 to 2, as said below
- top_coupling: float32 [8, 512, 512], P('tm', 'rows'), may hold values from -3 to 3
Outputs:
- sigma_diagonal: float32 [8, 512, 512], P('tm', 'rows')
- sigma_next: float32 [8, 512, 512], P('tm', 'rows')
- reduced_pivot: float32 [8, 512, 512], P('tm', 'rows')
The draws below stay inside these ranges and needn't reach their ends.
Inputs may be any that keep to these rules, and one draw needn't show every extreme that they name: `pivot_blocks`: each block is symmetric, and the block-tridiagonal matrix with these diagonal blocks and the couplings lower_blocks is positive definite. `top_diagonal`: each block is symmetric.
All inputs are finite; a program needn't handle non-finite values.
Results may differ from the reference program's by a relative error of at most 0.0001.
Values sent between devices are 32-bit elements; how exact they have to be, the bound alone decides.
No kernel may reach another device: no remote copies, remote signals or barrier semaphores. Data moves between devices by JAX's collectives and lax.ppermute only.
A program may use at most 64 MiB of HBM per device.

```python
import math
import jax
import jax.numpy as jnp
from jax import lax

B = 512
LEVELS = 2
PARTS_SIZE = 8


def symmetric_noise(key, strength):
    raw_values = jnp.clip(jax.random.normal(key, (PARTS_SIZE, B, B), jnp.float32), -4.0, 4.0)
    return (raw_values + jnp.swapaxes(raw_values, 1, 2)) * (0.5 * strength / jnp.sqrt(B * 1.0))


def field_weights(key):
    base_key = jax.random.fold_in(key, 71)
    mass_key, time_key, cross_key, bond_key = jax.random.split(base_key, 4)
    chain_mask = (jnp.arange(B) < B - 1).astype(jnp.float32)
    masses = jax.random.uniform(mass_key, (PARTS_SIZE, B), jnp.float32, 0.5, 1.0)
    time_low = math.log(1.0)
    time_weights = jnp.exp(jax.random.uniform(time_key, (PARTS_SIZE + 1, B), jnp.float32, time_low, math.log(4.0)))
    cross_weights = jnp.exp(jax.random.uniform(cross_key, (PARTS_SIZE + 1, B), jnp.float32, math.log(0.4), math.log(2.0))) * chain_mask[None, :]
    bond_weights = jnp.exp(jax.random.uniform(bond_key, (PARTS_SIZE, B), jnp.float32, math.log(0.3), math.log(3.0))) * chain_mask[None, :]
    return (masses, time_weights, cross_weights, bond_weights)


def draw_pivot_blocks(key, part):
    masses, time_weights, cross_weights, bond_weights = field_weights(key)
    noise_key = jax.random.fold_in(key, 11)
    cross_here = cross_weights[:PARTS_SIZE]
    cross_after = cross_weights[1:]
    diagonal = masses + time_weights[:PARTS_SIZE] + time_weights[1:] + bond_weights + jnp.roll(bond_weights, 1, axis=1)
    diagonal = diagonal + cross_here + jnp.roll(cross_here, 1, axis=1) + cross_after + jnp.roll(cross_after, 1, axis=1)
    identity = jnp.eye(B, dtype=jnp.float32)
    chain_part = jnp.eye(B, k=1, dtype=jnp.float32)[None] * (-bond_weights)[:, :, None]
    return symmetric_noise(noise_key, 0.05) + identity[None] * diagonal[:, None, :] + chain_part + jnp.swapaxes(chain_part, 1, 2)


def draw_lower_blocks(key, part):
    masses, time_weights, cross_weights, bond_weights = field_weights(key)
    noise_key = jax.random.fold_in(key, 37)
    raw_values = jnp.clip(jax.random.normal(noise_key, (PARTS_SIZE, B, B), jnp.float32), -4.0, 4.0)
    identity = jnp.eye(B, dtype=jnp.float32)
    upper_band = jnp.eye(B, k=1, dtype=jnp.float32)
    cross_here = cross_weights[:PARTS_SIZE]
    coupling = -(identity[None] * time_weights[:PARTS_SIZE][:, None, :])
    coupling = coupling - upper_band[None] * cross_here[:, :, None] - jnp.swapaxes(upper_band, 0, 1)[None] * cross_here[:, None, :]
    return coupling + raw_values * (0.03 / jnp.sqrt(B * 1.0))


def draw_top_diagonal(key, part):
    noise_key, scale_key = jax.random.split(jax.random.fold_in(key, 23))
    scales = jax.random.uniform(scale_key, (PARTS_SIZE, 1, B), jnp.float32, 0.5, 1.5)
    return symmetric_noise(noise_key, 0.5) + jnp.eye(B, dtype=jnp.float32)[None] * scales


def shard_levels(key, dims, cuts, low, top_value):
    def one(position, shards_of):
        heights = jax.random.uniform(jax.random.fold_in(jax.random.fold_in(key, 6), position), (shards_of,), jnp.float32, low / len(cuts), top_value / len(cuts))
        return jnp.repeat(jnp.exp(heights), dims[position] // shards_of).reshape((-1,) + (1,) * (len(dims) - position - 1))

    factor_of = one(*cuts[0])
    for cut in cuts[1:]:
        factor_of = factor_of * one(*cut)
    return factor_of


def scatter_about(stream_key, shape, spread, reach, pieces=(), held_as=jnp.bfloat16):
    values = jax.random.normal(stream_key, shape, jnp.float32) * spread
    if len(pieces) > 0:
        values = shard_levels(stream_key, shape, pieces, -0.22, 0.18) * values
    return jnp.clip(values, min=-reach, max=reach).astype(held_as)


def setup_inputs(seed: int = 0) -> dict:
    keys = jax.random.split(jax.random.key(seed), 5)
    return {
        "pivot_blocks": draw_pivot_blocks(jax.random.fold_in(keys[4], 71), 0),
        "lower_blocks": draw_lower_blocks(jax.random.fold_in(keys[4], 71), 0),
        "top_diagonal": draw_top_diagonal(jax.random.fold_in(keys[4], 71), 0),
        "top_coupling": scatter_about(keys[3], (PARTS_SIZE, B, B), 0.5, 3.0, ((0, 8), (1, 4)), jnp.float32),
    }


precise = lax.Precision.HIGHEST

def batch_product(left, right):
    return jnp.matmul(left, right, precision=precise)

def flipped(blocks):
    return jnp.swapaxes(blocks, 1, 2)

def solve_batch(factor, right_side):
    return jax.vmap(lambda single, given: jax.scipy.linalg.cho_solve((single, True), given))(factor, right_side)

def from_below(blocks, spacing):
    pad_blocks = jnp.zeros((spacing,) + blocks.shape[1:], jnp.float32)
    return jnp.concatenate([pad_blocks, blocks[:-spacing]], 0)

def from_above(blocks, spacing):
    pad_blocks = jnp.zeros((spacing,) + blocks.shape[1:], jnp.float32)
    return jnp.concatenate([blocks[spacing:], pad_blocks], 0)

def reference(pivot_blocks, lower_blocks, top_diagonal, top_coupling):
    parts_count = pivot_blocks.shape[0]
    full_width = pivot_blocks.shape[1]
    indices = jnp.arange(parts_count)
    empty = jnp.zeros((1, full_width, full_width), jnp.float32)
    lower_now = jnp.where((indices == 0)[:, None, None], jnp.float32(0.0), lower_blocks)
    upper_now = jnp.concatenate([flipped(lower_now[1:]), empty], 0)
    pivot_now = pivot_blocks
    identity = jnp.eye(full_width, dtype=jnp.float32)
    saved = []
    for tier_index in range(LEVELS):
        spacing = 2 ** tier_index
        factor = jnp.linalg.cholesky(pivot_now)
        left_solved = solve_batch(factor, lower_now)
        right_solved = solve_batch(factor, upper_now)
        inverse = solve_batch(factor, jnp.broadcast_to(identity, factor.shape))
        drop_left = batch_product(flipped(lower_now), left_solved)
        upper_new = -batch_product(flipped(left_solved), upper_now)
        drop_right = batch_product(flipped(upper_now), right_solved)
        lower_new = -batch_product(flipped(right_solved), lower_now)
        pivot_now = pivot_now - from_above(drop_left, spacing) - from_below(drop_right, spacing)
        upper_now = from_above(upper_new, spacing)
        lower_now = from_below(lower_new, spacing)
        saved.append((left_solved, right_solved, flipped(inverse)))
    reduced_pivot = pivot_now
    diagonal_now = top_diagonal
    next_now = jnp.where((indices + 2 ** LEVELS >= parts_count)[:, None, None], jnp.float32(0.0), top_coupling)
    for tier_index in reversed(range(LEVELS)):
        spacing = 2 ** tier_index
        left_solved, right_solved, inverse_now = saved[tier_index]
        near_diagonal = from_below(diagonal_now, spacing)
        near_next = from_below(next_now, spacing)
        far_diagonal = from_above(diagonal_now, spacing)
        cross_near = batch_product(left_solved, near_diagonal) + batch_product(right_solved, flipped(near_next))
        cross_far = batch_product(left_solved, near_next) + batch_product(right_solved, far_diagonal)
        diagonal_now = inverse_now + batch_product(cross_near, flipped(left_solved)) + batch_product(cross_far, flipped(right_solved))
        next_now = -cross_far
    next_now = jnp.where((indices == parts_count - 1)[:, None, None], jnp.float32(0.0), next_now)
    return (diagonal_now, next_now, reduced_pivot)
```

```python
import jax
import jax.numpy as jnp
from jax import lax
from jax.sharding import PartitionSpec as P
from jax.experimental import pallas as pl
from jax.experimental.pallas import tpu as pltpu

LEVELS = 2


precise = lax.Precision.HIGHEST


def passed_along(value, axis, steps):
    count = lax.axis_size(axis)
    leading, last = (max(0, -steps), min(count, count - steps))
    return lax.ppermute(value, axis, [(source, source + steps) for source in range(leading, last)])


def product(left, right):
    return jnp.dot(left, right, precision=precise, preferred_element_type=jnp.float32)


def product_flip(left, right):
    return lax.dot_general(
        left, right, (((1,), (1,)), ((), ())), precision=precise, preferred_element_type=jnp.float32
    )


def product_over(left, right):
    return lax.dot_general(
        left, right, (((0,), (0,)), ((), ())), precision=precise, preferred_element_type=jnp.float32
    )


def small_inverse(block):
    size = block.shape[0]
    sub = lax.broadcasted_iota(jnp.int32, (size, size), 0)
    lane = lax.broadcasted_iota(jnp.int32, (size, size), 1)
    sub_col = lax.broadcasted_iota(jnp.int32, (size, 1), 0)
    lane_row = lax.broadcasted_iota(jnp.int32, (1, size), 1)

    def step(k, held):
        row_mask = sub == k
        col_mask = lane == k
        row = jnp.sum(jnp.where(row_mask, held, 0.0), axis=0, keepdims=True)
        col = jnp.sum(jnp.where(col_mask, held, 0.0), axis=1, keepdims=True)
        pivot = jnp.sum(jnp.where(lane_row == k, row, 0.0), axis=1, keepdims=True)
        scaled = jnp.where(lane_row == k, 1.0, row) / pivot
        col = jnp.where(sub_col == k, 0.0, col)
        held = jnp.where(col_mask, 0.0, held) - col * scaled
        return jnp.where(row_mask, scaled, held)

    return lax.fori_loop(0, size, step, block)


def inverse_kernel(a_ref, o_ref):
    n = a_ref.shape[0]
    b = 128
    o_ref[...] = a_ref[...]
    sub_b = lax.broadcasted_iota(jnp.int32, (b, n), 0)
    lane_b = lax.broadcasted_iota(jnp.int32, (b, n), 1)
    sub_n = lax.broadcasted_iota(jnp.int32, (n, b), 0)
    lane_n = lax.broadcasted_iota(jnp.int32, (n, n), 1)
    for k in range(n // b):
        lo = k * b
        pivot_inv = small_inverse(o_ref[lo : lo + b, lo : lo + b])
        in_block = (lane_b >= lo) & (lane_b < lo + b)
        row_block = jnp.where(in_block, (lane_b - lo == sub_b).astype(jnp.float32), o_ref[lo : lo + b, :])
        row_new = jnp.dot(pivot_inv, row_block, precision=precise, preferred_element_type=jnp.float32)
        col_block = o_ref[:, lo : lo + b]
        col_block = jnp.where((sub_n >= lo) & (sub_n < lo + b), 0.0, col_block)
        whole = jnp.where((lane_n >= lo) & (lane_n < lo + b), 0.0, o_ref[...])
        o_ref[...] = whole - jnp.dot(col_block, row_new, precision=precise, preferred_element_type=jnp.float32)
        o_ref[lo : lo + b, :] = row_new


def spd_inverse(matrix):
    n = matrix.shape[0]
    return pl.pallas_call(
        inverse_kernel,
        out_shape=jax.ShapeDtypeStruct((n, n), jnp.float32),
        in_specs=[pl.BlockSpec(memory_space=pltpu.VMEM)],
        out_specs=pl.BlockSpec(memory_space=pltpu.VMEM),
        cost_estimate=pl.CostEstimate(flops=2 * n * n * n, bytes_accessed=8 * n * n, transcendentals=0),
    )(matrix)


def local(pivot_blocks, lower_blocks, top_diagonal, top_coupling):
    parts_count = lax.axis_size("tm")
    position = lax.axis_index("tm")
    row_part = lax.axis_index("rows")
    full_width = pivot_blocks.shape[1]
    quarter = lower_blocks.shape[2]
    row_start = row_part * quarter
    first_pivot = pivot_blocks[0]
    lower_columns = jnp.where(position == 0, jnp.zeros_like(lower_blocks[0]), lower_blocks[0])
    lower_rows = lax.all_to_all(lower_columns, "rows", split_axis=0, concat_axis=1, tiled=True)
    next_rows = passed_along(lower_rows, "tm", -1)
    upper_columns = next_rows.T
    pivot_rows = lax.dynamic_slice_in_dim(first_pivot, row_start, quarter, 0)
    saved = []
    for tier_index in range(LEVELS):
        spacing = 2**tier_index
        if tier_index == 0:
            whole_pivot = first_pivot
        else:
            whole_pivot = lax.all_gather(pivot_rows, "rows", axis=0, tiled=True)
        inverse_whole = spd_inverse(whole_pivot)
        solved = product(inverse_whole, jnp.concatenate([lower_columns, upper_columns], axis=1))
        left_columns = solved[:, :quarter]
        right_columns = solved[:, quarter : 2 * quarter]
        inverse_columns = lax.dynamic_slice_in_dim(inverse_whole, row_start, quarter, 1)
        left_solved, right_solved = (
            lax.all_gather(left_columns, "rows", axis=1, tiled=True),
            lax.all_gather(right_columns, "rows", axis=1, tiled=True),
        )
        drop_left = product_over(lower_columns, left_solved)
        upper_new = -product_over(upper_columns, left_solved)
        left_bound = passed_along(jnp.stack([drop_left, upper_new]), "tm", -spacing)
        drop_right = product_over(upper_columns, right_solved)
        lower_new = -product_over(lower_columns, right_solved)
        right_bound = passed_along(jnp.stack([drop_right, lower_new]), "tm", spacing)
        pivot_rows = pivot_rows - left_bound[0] - right_bound[0]
        upper_columns = left_bound[1].T
        lower_columns = right_bound[1].T
        saved.append((left_solved, right_solved, inverse_columns))
    diagonal_rows = top_diagonal[0]
    coupling_rows = jnp.where(
        position + 2**LEVELS >= parts_count, jnp.zeros_like(top_coupling[0]), top_coupling[0]
    )
    for tier_index in reversed(range(LEVELS)):
        spacing = 2**tier_index
        saved_left, saved_right, saved_inverse = saved[tier_index]
        left_rows = lax.dynamic_slice_in_dim(saved_left, row_start, quarter, 0)
        right_rows = lax.dynamic_slice_in_dim(saved_right, row_start, quarter, 0)
        from_left = passed_along(jnp.stack([diagonal_rows, coupling_rows]), "tm", spacing)
        from_right = passed_along(diagonal_rows, "tm", -spacing)
        joined = lax.all_gather(
            jnp.concatenate([from_left, from_right[None]], 0), "rows", axis=1, tiled=True
        )
        near_diagonal = joined[0]
        near_next = joined[1]
        far_diagonal = joined[2]
        cross_near = product(left_rows, near_diagonal) + product_flip(right_rows, near_next)
        cross_far = product(left_rows, near_next) + product(right_rows, far_diagonal)
        diagonal_rows = (
            saved_inverse.T
            + product_flip(cross_near, saved_left)
            + product_flip(cross_far, saved_right)
        )
        coupling_rows = -cross_far
    coupling_rows = jnp.where(
        position == parts_count - 1, jnp.zeros_like(coupling_rows), coupling_rows
    )
    return (diagonal_rows[None], coupling_rows[None], pivot_rows[None])


def solution(mesh):
    placed = (
        P("tm", None, None),
        P("tm", None, "rows"),
        P("tm", "rows", None),
        P("tm", "rows", None),
    )
    return jax.shard_map(
        local,
        mesh=mesh,
        in_specs=placed,
        out_specs=(P("tm", "rows", None), P("tm", "rows", None), P("tm", "rows", None)),
        check_vma=False,
    )
```

```python
import jax
import jax.numpy as jnp
from jax import lax
from jax.sharding import PartitionSpec as P
from jax.experimental import pallas as pl
from jax.experimental.pallas import tpu as pltpu

LEVELS = 2
LEAF = 32


precise = lax.Precision.HIGHEST


def passed_along(value, axis, steps):
    count = lax.axis_size(axis)
    leading, last = (max(0, -steps), min(count, count - steps))
    return lax.ppermute(value, axis, [(source, source + steps) for source in range(leading, last)])


def product(left, right):
    return jnp.dot(left, right, precision=precise, preferred_element_type=jnp.float32)


def product_flip(left, right):
    return lax.dot_general(
        left, right, (((1,), (1,)), ((), ())), precision=precise, preferred_element_type=jnp.float32
    )


def product_over(left, right):
    return lax.dot_general(
        left, right, (((0,), (0,)), ((), ())), precision=precise, preferred_element_type=jnp.float32
    )


def strip_inverse(strip, offset):
    rows, width = strip.shape
    sub = lax.broadcasted_iota(jnp.int32, (rows, width), 0)
    lane = lax.broadcasted_iota(jnp.int32, (rows, width), 1)
    sub_col = lax.broadcasted_iota(jnp.int32, (rows, 1), 0)
    lane_row = lax.broadcasted_iota(jnp.int32, (1, width), 1)
    inside = (lane >= offset) & (lane < offset + rows)

    def step(k, held):
        row_mask = sub == k
        col_mask = lane == k + offset
        row = jnp.sum(jnp.where(row_mask, held, 0.0), axis=0, keepdims=True)
        col = jnp.sum(jnp.where(col_mask, held, 0.0), axis=1, keepdims=True)
        pivot = jnp.sum(jnp.where(lane_row == k + offset, row, 0.0), axis=1, keepdims=True)
        scaled = jnp.where(lane_row == k + offset, 1.0, row) / pivot
        col = jnp.where(sub_col == k, 0.0, col)
        held = jnp.where(col_mask, 0.0, held) - col * scaled
        return jnp.where(row_mask, scaled, held)

    return lax.fori_loop(0, rows, step, jnp.where(inside, strip, 0.0))


def eliminate(held, low, size, row_base, inverse_strip):
    rows, width = held.shape
    sub = lax.broadcasted_iota(jnp.int32, (rows, width), 0)
    lane = lax.broadcasted_iota(jnp.int32, (rows, width), 1)
    lanes_in = (lane >= low) & (lane < low + size)
    rows_in = (sub >= low) & (sub < low + size)
    span = held[row_base : row_base + 128, :]
    span_sub = sub[row_base : row_base + 128, :]
    span_lane = lane[row_base : row_base + 128, :]
    span_rows = jnp.where(
        (span_lane >= low) & (span_lane < low + size),
        (span_lane == span_sub).astype(jnp.float32),
        span,
    )
    row_new = jnp.dot(inverse_strip, span_rows, precision=precise, preferred_element_type=jnp.float32)
    pieces = []
    if low - row_base > 0:
        pieces.append(jnp.zeros((low - row_base, width), jnp.float32))
    pieces.append(row_new)
    if row_base + 128 - low - size > 0:
        pieces.append(jnp.zeros((row_base + 128 - low - size, width), jnp.float32))
    placed = jnp.concatenate(pieces, axis=0) if len(pieces) > 1 else row_new
    col_base = (low // 128) * 128
    cols = held[:, col_base : col_base + 128]
    cols = jnp.where(lanes_in[:, col_base : col_base + 128] & ~rows_in[:, col_base : col_base + 128], cols, 0.0)
    held = jnp.where(lanes_in, 0.0, held) - jnp.dot(cols, placed, precision=precise, preferred_element_type=jnp.float32)
    return jnp.where(rows_in, jnp.concatenate([jnp.zeros((row_base, width), jnp.float32), placed, jnp.zeros((rows - row_base - 128, width), jnp.float32)], axis=0) if rows > 128 else placed, held)


def block_inverse(block, leaf):
    for j in range(block.shape[0] // leaf):
        low = j * leaf
        inverse_strip = strip_inverse(block[low : low + leaf, :], low)
        block = eliminate(block, low, leaf, 0, inverse_strip)
    return block


def inverse_kernel(a_ref, o_ref):
    n = a_ref.shape[0]
    b = 128
    o_ref[...] = a_ref[...]
    sub_b = lax.broadcasted_iota(jnp.int32, (b, n), 0)
    lane_b = lax.broadcasted_iota(jnp.int32, (b, n), 1)
    sub_n = lax.broadcasted_iota(jnp.int32, (n, b), 0)
    lane_n = lax.broadcasted_iota(jnp.int32, (n, n), 1)
    for k in range(n // b):
        lo = k * b
        pivot_inv = block_inverse(o_ref[lo : lo + b, lo : lo + b], LEAF)
        in_block = (lane_b >= lo) & (lane_b < lo + b)
        row_block = jnp.where(in_block, (lane_b - lo == sub_b).astype(jnp.float32), o_ref[lo : lo + b, :])
        row_new = jnp.dot(pivot_inv, row_block, precision=precise, preferred_element_type=jnp.float32)
        col_block = o_ref[:, lo : lo + b]
        col_block = jnp.where((sub_n >= lo) & (sub_n < lo + b), 0.0, col_block)
        whole = jnp.where((lane_n >= lo) & (lane_n < lo + b), 0.0, o_ref[...])
        o_ref[...] = whole - jnp.dot(col_block, row_new, precision=precise, preferred_element_type=jnp.float32)
        o_ref[lo : lo + b, :] = row_new


def spd_inverse(matrix):
    n = matrix.shape[0]
    return pl.pallas_call(
        inverse_kernel,
        out_shape=jax.ShapeDtypeStruct((n, n), jnp.float32),
        in_specs=[pl.BlockSpec(memory_space=pltpu.VMEM)],
        out_specs=pl.BlockSpec(memory_space=pltpu.VMEM),
        cost_estimate=pl.CostEstimate(flops=2 * n * n * n, bytes_accessed=8 * n * n, transcendentals=0),
    )(matrix)


def local(pivot_blocks, lower_blocks, top_diagonal, top_coupling):
    parts_count = lax.axis_size("tm")
    position = lax.axis_index("tm")
    row_part = lax.axis_index("rows")
    full_width = pivot_blocks.shape[1]
    quarter = lower_blocks.shape[2]
    row_start = row_part * quarter
    first_pivot = pivot_blocks[0]
    lower_columns = jnp.where(position == 0, jnp.zeros_like(lower_blocks[0]), lower_blocks[0])
    lower_rows = lax.all_to_all(lower_columns, "rows", split_axis=0, concat_axis=1, tiled=True)
    next_rows = passed_along(lower_rows, "tm", -1)
    upper_columns = next_rows.T
    pivot_rows = lax.dynamic_slice_in_dim(first_pivot, row_start, quarter, 0)
    saved = []
    for tier_index in range(LEVELS):
        spacing = 2**tier_index
        if tier_index == 0:
            whole_pivot = first_pivot
        else:
            whole_pivot = lax.all_gather(pivot_rows, "rows", axis=0, tiled=True)
        inverse_whole = spd_inverse(whole_pivot)
        solved = product(inverse_whole, jnp.concatenate([lower_columns, upper_columns], axis=1))
        left_columns = solved[:, :quarter]
        right_columns = solved[:, quarter : 2 * quarter]
        inverse_columns = lax.dynamic_slice_in_dim(inverse_whole, row_start, quarter, 1)
        left_solved, right_solved = (
            lax.all_gather(left_columns, "rows", axis=1, tiled=True),
            lax.all_gather(right_columns, "rows", axis=1, tiled=True),
        )
        drop_left = product_over(lower_columns, left_solved)
        upper_new = -product_over(upper_columns, left_solved)
        left_bound = passed_along(jnp.stack([drop_left, upper_new]), "tm", -spacing)
        drop_right = product_over(upper_columns, right_solved)
        lower_new = -product_over(lower_columns, right_solved)
        right_bound = passed_along(jnp.stack([drop_right, lower_new]), "tm", spacing)
        pivot_rows = pivot_rows - left_bound[0] - right_bound[0]
        upper_columns = left_bound[1].T
        lower_columns = right_bound[1].T
        saved.append((left_solved, right_solved, inverse_columns))
    diagonal_rows = top_diagonal[0]
    coupling_rows = jnp.where(
        position + 2**LEVELS >= parts_count, jnp.zeros_like(top_coupling[0]), top_coupling[0]
    )
    for tier_index in reversed(range(LEVELS)):
        spacing = 2**tier_index
        saved_left, saved_right, saved_inverse = saved[tier_index]
        left_rows = lax.dynamic_slice_in_dim(saved_left, row_start, quarter, 0)
        right_rows = lax.dynamic_slice_in_dim(saved_right, row_start, quarter, 0)
        from_left = passed_along(jnp.stack([diagonal_rows, coupling_rows]), "tm", spacing)
        from_right = passed_along(diagonal_rows, "tm", -spacing)
        joined = lax.all_gather(
            jnp.concatenate([from_left, from_right[None]], 0), "rows", axis=1, tiled=True
        )
        near_diagonal = joined[0]
        near_next = joined[1]
        far_diagonal = joined[2]
        cross_near = product(left_rows, near_diagonal) + product_flip(right_rows, near_next)
        cross_far = product(left_rows, near_next) + product(right_rows, far_diagonal)
        diagonal_rows = (
            saved_inverse.T
            + product_flip(cross_near, saved_left)
            + product_flip(cross_far, saved_right)
        )
        coupling_rows = -cross_far
    coupling_rows = jnp.where(
        position == parts_count - 1, jnp.zeros_like(coupling_rows), coupling_rows
    )
    return (diagonal_rows[None], coupling_rows[None], pivot_rows[None])


def solution(mesh):
    placed = (
        P("tm", None, None),
        P("tm", None, "rows"),
        P("tm", "rows", None),
        P("tm", "rows", None),
    )
    return jax.shard_map(
        local,
        mesh=mesh,
        in_specs=placed,
        out_specs=(P("tm", "rows", None), P("tm", "rows", None), P("tm", "rows", None)),
        check_vma=False,
    )
```

```python
import jax
import jax.numpy as jnp
from jax import lax
from jax.sharding import PartitionSpec as P
from jax.experimental import pallas as pl
from jax.experimental.pallas import tpu as pltpu

LEVELS = 2
LEAF = 32


precise = lax.Precision.HIGHEST


def passed_along(value, axis, steps):
    count = lax.axis_size(axis)
    leading, last = (max(0, -steps), min(count, count - steps))
    return lax.ppermute(value, axis, [(source, source + steps) for source in range(leading, last)])


def product(left, right):
    return jnp.dot(left, right, precision=precise, preferred_element_type=jnp.float32)


def product_flip(left, right):
    return lax.dot_general(
        left, right, (((1,), (1,)), ((), ())), precision=precise, preferred_element_type=jnp.float32
    )


def product_over(left, right):
    return lax.dot_general(
        left, right, (((0,), (0,)), ((), ())), precision=precise, preferred_element_type=jnp.float32
    )


def strip_inverse(strip, offset):
    rows, width = strip.shape
    sub = lax.broadcasted_iota(jnp.int32, (rows, width), 0)
    lane = lax.broadcasted_iota(jnp.int32, (rows, width), 1)
    sub_col = lax.broadcasted_iota(jnp.int32, (rows, 1), 0)
    lane_row = lax.broadcasted_iota(jnp.int32, (1, width), 1)
    inside = (lane >= offset) & (lane < offset + rows)

    def step(k, held):
        row_mask = sub == k
        col_mask = lane == k + offset
        row = jnp.sum(jnp.where(row_mask, held, 0.0), axis=0, keepdims=True)
        col = jnp.sum(jnp.where(col_mask, held, 0.0), axis=1, keepdims=True)
        pivot = jnp.sum(jnp.where(lane_row == k + offset, row, 0.0), axis=1, keepdims=True)
        scaled = jnp.where(lane_row == k + offset, 1.0, row) / pivot
        col = jnp.where(sub_col == k, 0.0, col)
        held = jnp.where(col_mask, 0.0, held) - col * scaled
        return jnp.where(row_mask, scaled, held)

    return lax.fori_loop(0, rows, step, jnp.where(inside, strip, 0.0))


def eliminate(held, low, size, row_base, inverse_strip):
    rows, width = held.shape
    sub = lax.broadcasted_iota(jnp.int32, (rows, width), 0)
    lane = lax.broadcasted_iota(jnp.int32, (rows, width), 1)
    lanes_in = (lane >= low) & (lane < low + size)
    rows_in = (sub >= low) & (sub < low + size)
    span = held[row_base : row_base + 128, :]
    span_sub = sub[row_base : row_base + 128, :]
    span_lane = lane[row_base : row_base + 128, :]
    span_rows = jnp.where(
        (span_lane >= low) & (span_lane < low + size),
        (span_lane == span_sub).astype(jnp.float32),
        span,
    )
    row_new = jnp.dot(inverse_strip, span_rows, precision=precise, preferred_element_type=jnp.float32)
    pieces = []
    if low - row_base > 0:
        pieces.append(jnp.zeros((low - row_base, width), jnp.float32))
    pieces.append(row_new)
    if row_base + 128 - low - size > 0:
        pieces.append(jnp.zeros((row_base + 128 - low - size, width), jnp.float32))
    placed = jnp.concatenate(pieces, axis=0) if len(pieces) > 1 else row_new
    col_base = (low // 128) * 128
    cols = held[:, col_base : col_base + 128]
    cols = jnp.where(lanes_in[:, col_base : col_base + 128] & ~rows_in[:, col_base : col_base + 128], cols, 0.0)
    held = jnp.where(lanes_in, 0.0, held) - jnp.dot(cols, placed, precision=precise, preferred_element_type=jnp.float32)
    return jnp.where(rows_in, jnp.concatenate([jnp.zeros((row_base, width), jnp.float32), placed, jnp.zeros((rows - row_base - 128, width), jnp.float32)], axis=0) if rows > 128 else placed, held)


def block_inverse(block, leaf):
    for j in range(block.shape[0] // leaf):
        low = j * leaf
        inverse_strip = strip_inverse(block[low : low + leaf, :], low)
        block = eliminate(block, low, leaf, 0, inverse_strip)
    return block


def inverse_kernel(a_ref, o_ref):
    n = a_ref.shape[0]
    b = 128
    o_ref[...] = a_ref[...]
    sub_b = lax.broadcasted_iota(jnp.int32, (b, n), 0)
    lane_b = lax.broadcasted_iota(jnp.int32, (b, n), 1)
    sub_n = lax.broadcasted_iota(jnp.int32, (n, b), 0)
    lane_n = lax.broadcasted_iota(jnp.int32, (n, n), 1)
    for k in range(n // b):
        lo = k * b
        pivot_inv = block_inverse(o_ref[lo : lo + b, lo : lo + b], LEAF)
        in_block = (lane_b >= lo) & (lane_b < lo + b)
        row_block = jnp.where(in_block, (lane_b - lo == sub_b).astype(jnp.float32), o_ref[lo : lo + b, :])
        row_new = jnp.dot(pivot_inv, row_block, precision=precise, preferred_element_type=jnp.float32)
        col_block = o_ref[:, lo : lo + b]
        col_block = jnp.where((sub_n >= lo) & (sub_n < lo + b), 0.0, col_block)
        whole = jnp.where((lane_n >= lo) & (lane_n < lo + b), 0.0, o_ref[...])
        o_ref[...] = whole - jnp.dot(col_block, row_new, precision=precise, preferred_element_type=jnp.float32)
        o_ref[lo : lo + b, :] = row_new


def spd_inverse(matrix):
    n = matrix.shape[0]
    return pl.pallas_call(
        inverse_kernel,
        out_shape=jax.ShapeDtypeStruct((n, n), jnp.float32),
        in_specs=[pl.BlockSpec(memory_space=pltpu.VMEM)],
        out_specs=pl.BlockSpec(memory_space=pltpu.VMEM),
        cost_estimate=pl.CostEstimate(flops=2 * n * n * n, bytes_accessed=8 * n * n, transcendentals=0),
    )(matrix)


def local(pivot_blocks, lower_blocks, top_diagonal, top_coupling):
    parts_count = lax.axis_size("tm")
    position = lax.axis_index("tm")
    row_part = lax.axis_index("rows")
    full_width = pivot_blocks.shape[1]
    quarter = lower_blocks.shape[2]
    row_start = row_part * quarter
    first_pivot = pivot_blocks[0]
    lower_columns = jnp.where(position == 0, jnp.zeros_like(lower_blocks[0]), lower_blocks[0])
    next_columns = passed_along(lower_columns, "tm", -1)
    lower_whole = lax.all_gather(lower_columns, "rows", axis=1, tiled=True)
    upper_whole = lax.all_gather(next_columns, "rows", axis=1, tiled=True).T
    upper_columns = lax.dynamic_slice_in_dim(upper_whole, row_start, quarter, 1)
    pivot_rows = lax.dynamic_slice_in_dim(first_pivot, row_start, quarter, 0)
    saved = []
    for tier_index in range(LEVELS):
        spacing = 2**tier_index
        if tier_index == 0:
            whole_pivot = first_pivot
        else:
            whole_pivot = lax.all_gather(pivot_rows, "rows", axis=0, tiled=True)
            lower_whole = lax.all_gather(lower_columns, "rows", axis=1, tiled=True)
            upper_whole = lax.all_gather(upper_columns, "rows", axis=1, tiled=True)
        inverse_whole = spd_inverse(whole_pivot)
        inverse_columns = lax.dynamic_slice_in_dim(inverse_whole, row_start, quarter, 1)
        left_solved = product(inverse_whole, lower_whole)
        right_solved = product(inverse_whole, upper_whole)
        drop_left = product_over(lower_columns, left_solved)
        upper_new = -product_over(upper_columns, left_solved)
        left_bound = passed_along(jnp.stack([drop_left, upper_new]), "tm", -spacing)
        drop_right = product_over(upper_columns, right_solved)
        lower_new = -product_over(lower_columns, right_solved)
        right_bound = passed_along(jnp.stack([drop_right, lower_new]), "tm", spacing)
        pivot_rows = pivot_rows - left_bound[0] - right_bound[0]
        upper_columns = left_bound[1].T
        lower_columns = right_bound[1].T
        saved.append((left_solved, right_solved, inverse_columns))
    diagonal_rows = top_diagonal[0]
    coupling_rows = jnp.where(
        position + 2**LEVELS >= parts_count, jnp.zeros_like(top_coupling[0]), top_coupling[0]
    )
    for tier_index in reversed(range(LEVELS)):
        spacing = 2**tier_index
        saved_left, saved_right, saved_inverse = saved[tier_index]
        left_rows = lax.dynamic_slice_in_dim(saved_left, row_start, quarter, 0)
        right_rows = lax.dynamic_slice_in_dim(saved_right, row_start, quarter, 0)
        from_left = passed_along(jnp.stack([diagonal_rows, coupling_rows]), "tm", spacing)
        from_right = passed_along(diagonal_rows, "tm", -spacing)
        joined = lax.all_gather(
            jnp.concatenate([from_left, from_right[None]], 0), "rows", axis=1, tiled=True
        )
        near_diagonal = joined[0]
        near_next = joined[1]
        far_diagonal = joined[2]
        cross_near = product(left_rows, near_diagonal) + product_flip(right_rows, near_next)
        cross_far = product(left_rows, near_next) + product(right_rows, far_diagonal)
        diagonal_rows = (
            saved_inverse.T
            + product_flip(cross_near, saved_left)
            + product_flip(cross_far, saved_right)
        )
        coupling_rows = -cross_far
    coupling_rows = jnp.where(
        position == parts_count - 1, jnp.zeros_like(coupling_rows), coupling_rows
    )
    return (diagonal_rows[None], coupling_rows[None], pivot_rows[None])


def solution(mesh):
    placed = (
        P("tm", None, None),
        P("tm", None, "rows"),
        P("tm", "rows", None),
        P("tm", "rows", None),
    )
    return jax.shard_map(
        local,
        mesh=mesh,
        in_specs=placed,
        out_specs=(P("tm", "rows", None), P("tm", "rows", None), P("tm", "rows", None)),
        check_vma=False,
    )
```

```python
import jax
import jax.numpy as jnp
from jax import lax
from jax.sharding import PartitionSpec as P
from jax.experimental import pallas as pl
from jax.experimental.pallas import tpu as pltpu

LEVELS = 2
LEAF = 32


precise = lax.Precision.HIGHEST


def passed_along(value, axis, steps):
    count = lax.axis_size(axis)
    leading, last = (max(0, -steps), min(count, count - steps))
    return lax.ppermute(value, axis, [(source, source + steps) for source in range(leading, last)])


def product(left, right):
    return jnp.dot(left, right, precision=precise, preferred_element_type=jnp.float32)


def product_flip(left, right):
    return lax.dot_general(
        left, right, (((1,), (1,)), ((), ())), precision=precise, preferred_element_type=jnp.float32
    )


def product_over(left, right):
    return lax.dot_general(
        left, right, (((0,), (0,)), ((), ())), precision=precise, preferred_element_type=jnp.float32
    )


def strip_inverse(strip, offset):
    rows, width = strip.shape
    sub = lax.broadcasted_iota(jnp.int32, (rows, width), 0)
    lane = lax.broadcasted_iota(jnp.int32, (rows, width), 1)
    sub_col = lax.broadcasted_iota(jnp.int32, (rows, 1), 0)
    lane_row = lax.broadcasted_iota(jnp.int32, (1, width), 1)
    inside = (lane >= offset) & (lane < offset + rows)

    def step(pair, held):
        k = 2 * pair
        first_row = sub == k
        second_row = sub == k + 1
        first_lane = lane == k + offset
        second_lane = lane == k + 1 + offset
        row_a = jnp.sum(jnp.where(first_row, held, 0.0), axis=0, keepdims=True)
        row_b = jnp.sum(jnp.where(second_row, held, 0.0), axis=0, keepdims=True)
        col_a = jnp.sum(jnp.where(first_lane, held, 0.0), axis=1, keepdims=True)
        col_b = jnp.sum(jnp.where(second_lane, held, 0.0), axis=1, keepdims=True)
        top_a = jnp.sum(jnp.where(sub_col == k, col_a, 0.0), axis=0, keepdims=True)
        low_a = jnp.sum(jnp.where(sub_col == k + 1, col_a, 0.0), axis=0, keepdims=True)
        top_b = jnp.sum(jnp.where(sub_col == k, col_b, 0.0), axis=0, keepdims=True)
        low_b = jnp.sum(jnp.where(sub_col == k + 1, col_b, 0.0), axis=0, keepdims=True)
        inv_det = 1.0 / (top_a * low_b - top_b * low_a)
        at_first = lane_row == k + offset
        at_second = lane_row == k + 1 + offset
        row_a = jnp.where(at_first, 1.0, jnp.where(at_second, 0.0, row_a))
        row_b = jnp.where(at_first, 0.0, jnp.where(at_second, 1.0, row_b))
        new_a = (low_b * row_a - top_b * row_b) * inv_det
        new_b = (top_a * row_b - low_a * row_a) * inv_det
        pivot_rows = (sub_col == k) | (sub_col == k + 1)
        col_a = jnp.where(pivot_rows, 0.0, col_a)
        col_b = jnp.where(pivot_rows, 0.0, col_b)
        held = jnp.where(first_lane | second_lane, 0.0, held) - col_a * new_a - col_b * new_b
        return jnp.where(first_row, new_a, jnp.where(second_row, new_b, held))

    return lax.fori_loop(0, rows // 2, step, jnp.where(inside, strip, 0.0))


def eliminate(held, low, size, row_base, inverse_strip):
    rows, width = held.shape
    sub = lax.broadcasted_iota(jnp.int32, (rows, width), 0)
    lane = lax.broadcasted_iota(jnp.int32, (rows, width), 1)
    lanes_in = (lane >= low) & (lane < low + size)
    rows_in = (sub >= low) & (sub < low + size)
    span = held[row_base : row_base + 128, :]
    span_sub = sub[row_base : row_base + 128, :]
    span_lane = lane[row_base : row_base + 128, :]
    span_rows = jnp.where(
        (span_lane >= low) & (span_lane < low + size),
        (span_lane == span_sub).astype(jnp.float32),
        span,
    )
    row_new = jnp.dot(inverse_strip, span_rows, precision=precise, preferred_element_type=jnp.float32)
    pieces = []
    if low - row_base > 0:
        pieces.append(jnp.zeros((low - row_base, width), jnp.float32))
    pieces.append(row_new)
    if row_base + 128 - low - size > 0:
        pieces.append(jnp.zeros((row_base + 128 - low - size, width), jnp.float32))
    placed = jnp.concatenate(pieces, axis=0) if len(pieces) > 1 else row_new
    col_base = (low // 128) * 128
    cols = held[:, col_base : col_base + 128]
    cols = jnp.where(lanes_in[:, col_base : col_base + 128] & ~rows_in[:, col_base : col_base + 128], cols, 0.0)
    held = jnp.where(lanes_in, 0.0, held) - jnp.dot(cols, placed, precision=precise, preferred_element_type=jnp.float32)
    return jnp.where(rows_in, jnp.concatenate([jnp.zeros((row_base, width), jnp.float32), placed, jnp.zeros((rows - row_base - 128, width), jnp.float32)], axis=0) if rows > 128 else placed, held)


def block_inverse(block, leaf):
    for j in range(block.shape[0] // leaf):
        low = j * leaf
        inverse_strip = strip_inverse(block[low : low + leaf, :], low)
        block = eliminate(block, low, leaf, 0, inverse_strip)
    return block


def inverse_kernel(a_ref, o_ref):
    n = a_ref.shape[0]
    b = 128
    o_ref[...] = a_ref[...]
    sub_b = lax.broadcasted_iota(jnp.int32, (b, n), 0)
    lane_b = lax.broadcasted_iota(jnp.int32, (b, n), 1)
    sub_n = lax.broadcasted_iota(jnp.int32, (n, b), 0)
    lane_n = lax.broadcasted_iota(jnp.int32, (n, n), 1)
    for k in range(n // b):
        lo = k * b
        pivot_inv = block_inverse(o_ref[lo : lo + b, lo : lo + b], LEAF)
        in_block = (lane_b >= lo) & (lane_b < lo + b)
        row_block = jnp.where(in_block, (lane_b - lo == sub_b).astype(jnp.float32), o_ref[lo : lo + b, :])
        row_new = jnp.dot(pivot_inv, row_block, precision=precise, preferred_element_type=jnp.float32)
        col_block = o_ref[:, lo : lo + b]
        col_block = jnp.where((sub_n >= lo) & (sub_n < lo + b), 0.0, col_block)
        whole = jnp.where((lane_n >= lo) & (lane_n < lo + b), 0.0, o_ref[...])
        o_ref[...] = whole - jnp.dot(col_block, row_new, precision=precise, preferred_element_type=jnp.float32)
        o_ref[lo : lo + b, :] = row_new


def spd_inverse(matrix):
    n = matrix.shape[0]
    return pl.pallas_call(
        inverse_kernel,
        out_shape=jax.ShapeDtypeStruct((n, n), jnp.float32),
        in_specs=[pl.BlockSpec(memory_space=pltpu.VMEM)],
        out_specs=pl.BlockSpec(memory_space=pltpu.VMEM),
        cost_estimate=pl.CostEstimate(flops=2 * n * n * n, bytes_accessed=8 * n * n, transcendentals=0),
    )(matrix)


def local(pivot_blocks, lower_blocks, top_diagonal, top_coupling):
    parts_count = lax.axis_size("tm")
    position = lax.axis_index("tm")
    row_part = lax.axis_index("rows")
    full_width = pivot_blocks.shape[1]
    quarter = lower_blocks.shape[2]
    row_start = row_part * quarter
    first_pivot = pivot_blocks[0]
    lower_columns = jnp.where(position == 0, jnp.zeros_like(lower_blocks[0]), lower_blocks[0])
    next_columns = passed_along(lower_columns, "tm", -1)
    lower_whole = lax.all_gather(lower_columns, "rows", axis=1, tiled=True)
    upper_whole = lax.all_gather(next_columns, "rows", axis=1, tiled=True).T
    upper_columns = lax.dynamic_slice_in_dim(upper_whole, row_start, quarter, 1)
    pivot_rows = lax.dynamic_slice_in_dim(first_pivot, row_start, quarter, 0)
    saved = []
    for tier_index in range(LEVELS):
        spacing = 2**tier_index
        if tier_index == 0:
            whole_pivot = first_pivot
        else:
            whole_pivot = lax.all_gather(pivot_rows, "rows", axis=0, tiled=True)
            lower_whole = lax.all_gather(lower_columns, "rows", axis=1, tiled=True)
            upper_whole = lax.all_gather(upper_columns, "rows", axis=1, tiled=True)
        inverse_whole = spd_inverse(whole_pivot)
        inverse_columns = lax.dynamic_slice_in_dim(inverse_whole, row_start, quarter, 1)
        left_solved = product(inverse_whole, lower_whole)
        right_solved = product(inverse_whole, upper_whole)
        drop_left = product_over(lower_columns, left_solved)
        upper_new = -product_over(upper_columns, left_solved)
        left_bound = passed_along(jnp.stack([drop_left, upper_new]), "tm", -spacing)
        drop_right = product_over(upper_columns, right_solved)
        lower_new = -product_over(lower_columns, right_solved)
        right_bound = passed_along(jnp.stack([drop_right, lower_new]), "tm", spacing)
        pivot_rows = pivot_rows - left_bound[0] - right_bound[0]
        upper_columns = left_bound[1].T
        lower_columns = right_bound[1].T
        saved.append((left_solved, right_solved, inverse_columns))
    diagonal_rows = top_diagonal[0]
    coupling_rows = jnp.where(
        position + 2**LEVELS >= parts_count, jnp.zeros_like(top_coupling[0]), top_coupling[0]
    )
    for tier_index in reversed(range(LEVELS)):
        spacing = 2**tier_index
        saved_left, saved_right, saved_inverse = saved[tier_index]
        left_rows = lax.dynamic_slice_in_dim(saved_left, row_start, quarter, 0)
        right_rows = lax.dynamic_slice_in_dim(saved_right, row_start, quarter, 0)
        from_left = passed_along(jnp.stack([diagonal_rows, coupling_rows]), "tm", spacing)
        from_right = passed_along(diagonal_rows, "tm", -spacing)
        joined = lax.all_gather(
            jnp.concatenate([from_left, from_right[None]], 0), "rows", axis=1, tiled=True
        )
        near_diagonal = joined[0]
        near_next = joined[1]
        far_diagonal = joined[2]
        cross_near = product(left_rows, near_diagonal) + product_flip(right_rows, near_next)
        cross_far = product(left_rows, near_next) + product(right_rows, far_diagonal)
        diagonal_rows = (
            saved_inverse.T
            + product_flip(cross_near, saved_left)
            + product_flip(cross_far, saved_right)
        )
        coupling_rows = -cross_far
    coupling_rows = jnp.where(
        position == parts_count - 1, jnp.zeros_like(coupling_rows), coupling_rows
    )
    return (diagonal_rows[None], coupling_rows[None], pivot_rows[None])


def solution(mesh):
    placed = (
        P("tm", None, None),
        P("tm", None, "rows"),
        P("tm", "rows", None),
        P("tm", "rows", None),
    )
    return jax.shard_map(
        local,
        mesh=mesh,
        in_specs=placed,
        out_specs=(P("tm", "rows", None), P("tm", "rows", None), P("tm", "rows", None)),
        check_vma=False,
    )
```

```python
import jax
import jax.numpy as jnp
from jax import lax
from jax.sharding import PartitionSpec as P
from jax.experimental import pallas as pl
from jax.experimental.pallas import tpu as pltpu

LEVELS = 2
LEAF = 32


precise = lax.Precision.HIGHEST


def passed_along(value, axis, steps):
    count = lax.axis_size(axis)
    leading, last = (max(0, -steps), min(count, count - steps))
    return lax.ppermute(value, axis, [(source, source + steps) for source in range(leading, last)])


def gather_rows(piece, axis):
    count = lax.axis_size("rows")
    me = lax.axis_index("rows")
    got = [piece] + [
        lax.ppermute(piece, "rows", [(i, (i + s) % count) for i in range(count)])
        for s in range(1, count)
    ]
    order = got[::-1]
    ordered = lax.dynamic_slice_in_dim(jnp.stack(order + order), (count - 1 - me) % count, count, 0)
    return jnp.concatenate([ordered[k] for k in range(count)], axis=axis)


def product(left, right):
    return jnp.dot(left, right, precision=precise, preferred_element_type=jnp.float32)


def product_flip(left, right):
    return lax.dot_general(
        left, right, (((1,), (1,)), ((), ())), precision=precise, preferred_element_type=jnp.float32
    )


def product_over(left, right):
    return lax.dot_general(
        left, right, (((0,), (0,)), ((), ())), precision=precise, preferred_element_type=jnp.float32
    )


def strip_inverse(strip, offset):
    rows, width = strip.shape
    sub = lax.broadcasted_iota(jnp.int32, (rows, width), 0)
    lane = lax.broadcasted_iota(jnp.int32, (rows, width), 1)
    sub_col = lax.broadcasted_iota(jnp.int32, (rows, 1), 0)
    lane_row = lax.broadcasted_iota(jnp.int32, (1, width), 1)
    inside = (lane >= offset) & (lane < offset + rows)

    def step(pair, held):
        k = 2 * pair
        first_row = sub == k
        second_row = sub == k + 1
        first_lane = lane == k + offset
        second_lane = lane == k + 1 + offset
        row_a = jnp.sum(jnp.where(first_row, held, 0.0), axis=0, keepdims=True)
        row_b = jnp.sum(jnp.where(second_row, held, 0.0), axis=0, keepdims=True)
        col_a = jnp.sum(jnp.where(first_lane, held, 0.0), axis=1, keepdims=True)
        col_b = jnp.sum(jnp.where(second_lane, held, 0.0), axis=1, keepdims=True)
        top_a = jnp.sum(jnp.where(sub_col == k, col_a, 0.0), axis=0, keepdims=True)
        low_a = jnp.sum(jnp.where(sub_col == k + 1, col_a, 0.0), axis=0, keepdims=True)
        top_b = jnp.sum(jnp.where(sub_col == k, col_b, 0.0), axis=0, keepdims=True)
        low_b = jnp.sum(jnp.where(sub_col == k + 1, col_b, 0.0), axis=0, keepdims=True)
        inv_det = 1.0 / (top_a * low_b - top_b * low_a)
        at_first = lane_row == k + offset
        at_second = lane_row == k + 1 + offset
        row_a = jnp.where(at_first, 1.0, jnp.where(at_second, 0.0, row_a))
        row_b = jnp.where(at_first, 0.0, jnp.where(at_second, 1.0, row_b))
        new_a = (low_b * row_a - top_b * row_b) * inv_det
        new_b = (top_a * row_b - low_a * row_a) * inv_det
        pivot_rows = (sub_col == k) | (sub_col == k + 1)
        col_a = jnp.where(pivot_rows, 0.0, col_a)
        col_b = jnp.where(pivot_rows, 0.0, col_b)
        held = jnp.where(first_lane | second_lane, 0.0, held) - col_a * new_a - col_b * new_b
        return jnp.where(first_row, new_a, jnp.where(second_row, new_b, held))

    return lax.fori_loop(0, rows // 2, step, jnp.where(inside, strip, 0.0))


def eliminate(held, low, size, row_base, inverse_strip):
    rows, width = held.shape
    sub = lax.broadcasted_iota(jnp.int32, (rows, width), 0)
    lane = lax.broadcasted_iota(jnp.int32, (rows, width), 1)
    lanes_in = (lane >= low) & (lane < low + size)
    rows_in = (sub >= low) & (sub < low + size)
    span = held[row_base : row_base + 128, :]
    span_sub = sub[row_base : row_base + 128, :]
    span_lane = lane[row_base : row_base + 128, :]
    span_rows = jnp.where(
        (span_lane >= low) & (span_lane < low + size),
        (span_lane == span_sub).astype(jnp.float32),
        span,
    )
    row_new = jnp.dot(inverse_strip, span_rows, precision=precise, preferred_element_type=jnp.float32)
    pieces = []
    if low - row_base > 0:
        pieces.append(jnp.zeros((low - row_base, width), jnp.float32))
    pieces.append(row_new)
    if row_base + 128 - low - size > 0:
        pieces.append(jnp.zeros((row_base + 128 - low - size, width), jnp.float32))
    placed = jnp.concatenate(pieces, axis=0) if len(pieces) > 1 else row_new
    col_base = (low // 128) * 128
    cols = held[:, col_base : col_base + 128]
    cols = jnp.where(lanes_in[:, col_base : col_base + 128] & ~rows_in[:, col_base : col_base + 128], cols, 0.0)
    held = jnp.where(lanes_in, 0.0, held) - jnp.dot(cols, placed, precision=precise, preferred_element_type=jnp.float32)
    return jnp.where(rows_in, jnp.concatenate([jnp.zeros((row_base, width), jnp.float32), placed, jnp.zeros((rows - row_base - 128, width), jnp.float32)], axis=0) if rows > 128 else placed, held)


def block_inverse(block, leaf):
    for j in range(block.shape[0] // leaf):
        low = j * leaf
        inverse_strip = strip_inverse(block[low : low + leaf, :], low)
        block = eliminate(block, low, leaf, 0, inverse_strip)
    return block


def inverse_kernel(a_ref, o_ref):
    n = a_ref.shape[0]
    b = 128
    o_ref[...] = a_ref[...]
    sub_b = lax.broadcasted_iota(jnp.int32, (b, n), 0)
    lane_b = lax.broadcasted_iota(jnp.int32, (b, n), 1)
    sub_n = lax.broadcasted_iota(jnp.int32, (n, b), 0)
    lane_n = lax.broadcasted_iota(jnp.int32, (n, n), 1)
    for k in range(n // b):
        lo = k * b
        pivot_inv = block_inverse(o_ref[lo : lo + b, lo : lo + b], LEAF)
        in_block = (lane_b >= lo) & (lane_b < lo + b)
        row_block = jnp.where(in_block, (lane_b - lo == sub_b).astype(jnp.float32), o_ref[lo : lo + b, :])
        row_new = jnp.dot(pivot_inv, row_block, precision=precise, preferred_element_type=jnp.float32)
        col_block = o_ref[:, lo : lo + b]
        col_block = jnp.where((sub_n >= lo) & (sub_n < lo + b), 0.0, col_block)
        whole = jnp.where((lane_n >= lo) & (lane_n < lo + b), 0.0, o_ref[...])
        o_ref[...] = whole - jnp.dot(col_block, row_new, precision=precise, preferred_element_type=jnp.float32)
        o_ref[lo : lo + b, :] = row_new


def spd_inverse(matrix):
    n = matrix.shape[0]
    return pl.pallas_call(
        inverse_kernel,
        out_shape=jax.ShapeDtypeStruct((n, n), jnp.float32),
        in_specs=[pl.BlockSpec(memory_space=pltpu.VMEM)],
        out_specs=pl.BlockSpec(memory_space=pltpu.VMEM),
        cost_estimate=pl.CostEstimate(flops=2 * n * n * n, bytes_accessed=8 * n * n, transcendentals=0),
    )(matrix)


def local(pivot_blocks, lower_blocks, top_diagonal, top_coupling):
    parts_count = lax.axis_size("tm")
    position = lax.axis_index("tm")
    row_part = lax.axis_index("rows")
    full_width = pivot_blocks.shape[1]
    quarter = lower_blocks.shape[2]
    row_start = row_part * quarter
    first_pivot = pivot_blocks[0]
    lower_columns = jnp.where(position == 0, jnp.zeros_like(lower_blocks[0]), lower_blocks[0])
    lower_whole = gather_rows(lower_columns, 1)
    with jax.named_scope("shift_next"):
        upper_whole = passed_along(lower_whole, "tm", -1).T
    upper_columns = lax.dynamic_slice_in_dim(upper_whole, row_start, quarter, 1)
    pivot_rows = lax.dynamic_slice_in_dim(first_pivot, row_start, quarter, 0)
    saved = []
    for tier_index in range(LEVELS):
        spacing = 2**tier_index
        if tier_index == 0:
            whole_pivot = first_pivot
        else:
            whole_pivot = gather_rows(pivot_rows, 0)
            with jax.named_scope("gather_couplings"):
                lower_whole = gather_rows(lower_columns, 1)
                upper_whole = gather_rows(upper_columns, 1)
        with jax.named_scope(f"inverse_{tier_index}"):
            inverse_whole = spd_inverse(whole_pivot)
        inverse_columns = lax.dynamic_slice_in_dim(inverse_whole, row_start, quarter, 1)
        left_solved = product(inverse_whole, lower_whole)
        right_solved = product(inverse_whole, upper_whole)
        drop_left = product_over(lower_columns, left_solved)
        upper_new = -product_over(upper_columns, left_solved)
        left_bound = passed_along(jnp.stack([drop_left, upper_new]), "tm", -spacing)
        drop_right = product_over(upper_columns, right_solved)
        lower_new = -product_over(lower_columns, right_solved)
        right_bound = passed_along(jnp.stack([drop_right, lower_new]), "tm", spacing)
        pivot_rows = pivot_rows - left_bound[0] - right_bound[0]
        upper_columns = left_bound[1].T
        lower_columns = right_bound[1].T
        saved.append((left_solved, right_solved, inverse_columns))
    diagonal_rows = top_diagonal[0]
    coupling_rows = jnp.where(
        position + 2**LEVELS >= parts_count, jnp.zeros_like(top_coupling[0]), top_coupling[0]
    )
    for tier_index in reversed(range(LEVELS)):
        spacing = 2**tier_index
        saved_left, saved_right, saved_inverse = saved[tier_index]
        left_rows = lax.dynamic_slice_in_dim(saved_left, row_start, quarter, 0)
        right_rows = lax.dynamic_slice_in_dim(saved_right, row_start, quarter, 0)
        from_left = passed_along(jnp.stack([diagonal_rows, coupling_rows]), "tm", spacing)
        from_right = passed_along(diagonal_rows, "tm", -spacing)
        joined = gather_rows(jnp.concatenate([from_left, from_right[None]], 0), 1)
        near_diagonal = joined[0]
        near_next = joined[1]
        far_diagonal = joined[2]
        cross_near = product(left_rows, near_diagonal) + product_flip(right_rows, near_next)
        cross_far = product(left_rows, near_next) + product(right_rows, far_diagonal)
        diagonal_rows = (
            saved_inverse.T
            + product_flip(cross_near, saved_left)
            + product_flip(cross_far, saved_right)
        )
        coupling_rows = -cross_far
    coupling_rows = jnp.where(
        position == parts_count - 1, jnp.zeros_like(coupling_rows), coupling_rows
    )
    return (diagonal_rows[None], coupling_rows[None], pivot_rows[None])


def solution(mesh):
    placed = (
        P("tm", None, None),
        P("tm", None, "rows"),
        P("tm", "rows", None),
        P("tm", "rows", None),
    )
    return jax.shard_map(
        local,
        mesh=mesh,
        in_specs=placed,
        out_specs=(P("tm", "rows", None), P("tm", "rows", None), P("tm", "rows", None)),
        check_vma=False,
    )
```

```python
import jax
import jax.numpy as jnp
from jax import lax
from jax.sharding import PartitionSpec as P
from jax.experimental import pallas as pl
from jax.experimental.pallas import tpu as pltpu

LEVELS = 2
LEAF = 32


precise = lax.Precision.HIGHEST
near = lax.Precision.HIGH


def passed_along(value, axis, steps):
    count = lax.axis_size(axis)
    leading, last = (max(0, -steps), min(count, count - steps))
    return lax.ppermute(value, axis, [(source, source + steps) for source in range(leading, last)])


def product(left, right):
    return jnp.dot(left, right, precision=near, preferred_element_type=jnp.float32)


def product_flip(left, right):
    return lax.dot_general(
        left, right, (((1,), (1,)), ((), ())), precision=near, preferred_element_type=jnp.float32
    )


def product_over(left, right):
    return lax.dot_general(
        left, right, (((0,), (0,)), ((), ())), precision=near, preferred_element_type=jnp.float32
    )


def strip_inverse(strip, offset):
    rows, width = strip.shape
    sub = lax.broadcasted_iota(jnp.int32, (rows, width), 0)
    lane = lax.broadcasted_iota(jnp.int32, (rows, width), 1)
    sub_col = lax.broadcasted_iota(jnp.int32, (rows, 1), 0)
    lane_row = lax.broadcasted_iota(jnp.int32, (1, width), 1)
    inside = (lane >= offset) & (lane < offset + rows)

    def step(pair, held):
        k = 2 * pair
        first_row = sub == k
        second_row = sub == k + 1
        first_lane = lane == k + offset
        second_lane = lane == k + 1 + offset
        row_a = jnp.sum(jnp.where(first_row, held, 0.0), axis=0, keepdims=True)
        row_b = jnp.sum(jnp.where(second_row, held, 0.0), axis=0, keepdims=True)
        col_a = jnp.sum(jnp.where(first_lane, held, 0.0), axis=1, keepdims=True)
        col_b = jnp.sum(jnp.where(second_lane, held, 0.0), axis=1, keepdims=True)
        top_a = jnp.sum(jnp.where(sub_col == k, col_a, 0.0), axis=0, keepdims=True)
        low_a = jnp.sum(jnp.where(sub_col == k + 1, col_a, 0.0), axis=0, keepdims=True)
        top_b = jnp.sum(jnp.where(sub_col == k, col_b, 0.0), axis=0, keepdims=True)
        low_b = jnp.sum(jnp.where(sub_col == k + 1, col_b, 0.0), axis=0, keepdims=True)
        inv_det = 1.0 / (top_a * low_b - top_b * low_a)
        at_first = lane_row == k + offset
        at_second = lane_row == k + 1 + offset
        row_a = jnp.where(at_first, 1.0, jnp.where(at_second, 0.0, row_a))
        row_b = jnp.where(at_first, 0.0, jnp.where(at_second, 1.0, row_b))
        new_a = (low_b * row_a - top_b * row_b) * inv_det
        new_b = (top_a * row_b - low_a * row_a) * inv_det
        pivot_rows = (sub_col == k) | (sub_col == k + 1)
        col_a = jnp.where(pivot_rows, 0.0, col_a)
        col_b = jnp.where(pivot_rows, 0.0, col_b)
        held = jnp.where(first_lane | second_lane, 0.0, held) - col_a * new_a - col_b * new_b
        return jnp.where(first_row, new_a, jnp.where(second_row, new_b, held))

    return lax.fori_loop(0, rows // 2, step, jnp.where(inside, strip, 0.0))


def eliminate(held, low, size, row_base, inverse_strip):
    rows, width = held.shape
    sub = lax.broadcasted_iota(jnp.int32, (rows, width), 0)
    lane = lax.broadcasted_iota(jnp.int32, (rows, width), 1)
    lanes_in = (lane >= low) & (lane < low + size)
    rows_in = (sub >= low) & (sub < low + size)
    span = held[row_base : row_base + 128, :]
    span_sub = sub[row_base : row_base + 128, :]
    span_lane = lane[row_base : row_base + 128, :]
    span_rows = jnp.where(
        (span_lane >= low) & (span_lane < low + size),
        (span_lane == span_sub).astype(jnp.float32),
        span,
    )
    row_new = jnp.dot(inverse_strip, span_rows, precision=precise, preferred_element_type=jnp.float32)
    pieces = []
    if low - row_base > 0:
        pieces.append(jnp.zeros((low - row_base, width), jnp.float32))
    pieces.append(row_new)
    if row_base + 128 - low - size > 0:
        pieces.append(jnp.zeros((row_base + 128 - low - size, width), jnp.float32))
    placed = jnp.concatenate(pieces, axis=0) if len(pieces) > 1 else row_new
    col_base = (low // 128) * 128
    cols = held[:, col_base : col_base + 128]
    cols = jnp.where(lanes_in[:, col_base : col_base + 128] & ~rows_in[:, col_base : col_base + 128], cols, 0.0)
    held = jnp.where(lanes_in, 0.0, held) - jnp.dot(cols, placed, precision=precise, preferred_element_type=jnp.float32)
    return jnp.where(rows_in, jnp.concatenate([jnp.zeros((row_base, width), jnp.float32), placed, jnp.zeros((rows - row_base - 128, width), jnp.float32)], axis=0) if rows > 128 else placed, held)


def block_inverse(block, leaf):
    for j in range(block.shape[0] // leaf):
        low = j * leaf
        inverse_strip = strip_inverse(block[low : low + leaf, :], low)
        block = eliminate(block, low, leaf, 0, inverse_strip)
    return block


def inverse_kernel(a_ref, o_ref):
    n = a_ref.shape[0]
    b = 128
    o_ref[...] = a_ref[...]
    sub_b = lax.broadcasted_iota(jnp.int32, (b, n), 0)
    lane_b = lax.broadcasted_iota(jnp.int32, (b, n), 1)
    sub_n = lax.broadcasted_iota(jnp.int32, (n, b), 0)
    lane_n = lax.broadcasted_iota(jnp.int32, (n, n), 1)
    for k in range(n // b):
        lo = k * b
        pivot_inv = block_inverse(o_ref[lo : lo + b, lo : lo + b], LEAF)
        in_block = (lane_b >= lo) & (lane_b < lo + b)
        row_block = jnp.where(in_block, (lane_b - lo == sub_b).astype(jnp.float32), o_ref[lo : lo + b, :])
        row_new = jnp.dot(pivot_inv, row_block, precision=precise, preferred_element_type=jnp.float32)
        col_block = o_ref[:, lo : lo + b]
        col_block = jnp.where((sub_n >= lo) & (sub_n < lo + b), 0.0, col_block)
        whole = jnp.where((lane_n >= lo) & (lane_n < lo + b), 0.0, o_ref[...])
        o_ref[...] = whole - jnp.dot(col_block, row_new, precision=precise, preferred_element_type=jnp.float32)
        o_ref[lo : lo + b, :] = row_new


def spd_inverse(matrix):
    n = matrix.shape[0]
    return pl.pallas_call(
        inverse_kernel,
        out_shape=jax.ShapeDtypeStruct((n, n), jnp.float32),
        in_specs=[pl.BlockSpec(memory_space=pltpu.VMEM)],
        out_specs=pl.BlockSpec(memory_space=pltpu.VMEM),
        cost_estimate=pl.CostEstimate(flops=2 * n * n * n, bytes_accessed=8 * n * n, transcendentals=0),
    )(matrix)


def local(pivot_blocks, lower_blocks, top_diagonal, top_coupling):
    parts_count = lax.axis_size("tm")
    position = lax.axis_index("tm")
    row_part = lax.axis_index("rows")
    full_width = pivot_blocks.shape[1]
    quarter = lower_blocks.shape[2]
    row_start = row_part * quarter
    first_pivot = pivot_blocks[0]
    lower_columns = jnp.where(position == 0, jnp.zeros_like(lower_blocks[0]), lower_blocks[0])
    next_columns = passed_along(lower_columns, "tm", -1)
    lower_whole = lax.all_gather(lower_columns, "rows", axis=1, tiled=True)
    upper_whole = lax.all_gather(next_columns, "rows", axis=1, tiled=True).T
    upper_columns = lax.dynamic_slice_in_dim(upper_whole, row_start, quarter, 1)
    pivot_rows = lax.dynamic_slice_in_dim(first_pivot, row_start, quarter, 0)
    saved = []
    for tier_index in range(LEVELS):
        spacing = 2**tier_index
        if tier_index == 0:
            whole_pivot = first_pivot
        else:
            whole_pivot = lax.all_gather(pivot_rows, "rows", axis=0, tiled=True)
            lower_whole = lax.all_gather(lower_columns, "rows", axis=1, tiled=True)
            upper_whole = lax.all_gather(upper_columns, "rows", axis=1, tiled=True)
        inverse_whole = spd_inverse(whole_pivot)
        inverse_columns = lax.dynamic_slice_in_dim(inverse_whole, row_start, quarter, 1)
        left_solved = product(inverse_whole, lower_whole)
        right_solved = product(inverse_whole, upper_whole)
        drop_left = product_over(lower_columns, left_solved)
        upper_new = -product_over(upper_columns, left_solved)
        left_bound = passed_along(jnp.stack([drop_left, upper_new]), "tm", -spacing)
        drop_right = product_over(upper_columns, right_solved)
        lower_new = -product_over(lower_columns, right_solved)
        right_bound = passed_along(jnp.stack([drop_right, lower_new]), "tm", spacing)
        pivot_rows = pivot_rows - left_bound[0] - right_bound[0]
        upper_columns = left_bound[1].T
        lower_columns = right_bound[1].T
        saved.append((left_solved, right_solved, inverse_columns))
    diagonal_rows = top_diagonal[0]
    coupling_rows = jnp.where(
        position + 2**LEVELS >= parts_count, jnp.zeros_like(top_coupling[0]), top_coupling[0]
    )
    for tier_index in reversed(range(LEVELS)):
        spacing = 2**tier_index
        saved_left, saved_right, saved_inverse = saved[tier_index]
        left_rows = lax.dynamic_slice_in_dim(saved_left, row_start, quarter, 0)
        right_rows = lax.dynamic_slice_in_dim(saved_right, row_start, quarter, 0)
        from_left = passed_along(jnp.stack([diagonal_rows, coupling_rows]), "tm", spacing)
        from_right = passed_along(diagonal_rows, "tm", -spacing)
        joined = lax.all_gather(
            jnp.concatenate([from_left, from_right[None]], 0), "rows", axis=1, tiled=True
        )
        near_diagonal = joined[0]
        near_next = joined[1]
        far_diagonal = joined[2]
        cross_near = product(left_rows, near_diagonal) + product_flip(right_rows, near_next)
        cross_far = product(left_rows, near_next) + product(right_rows, far_diagonal)
        diagonal_rows = (
            saved_inverse.T
            + product_flip(cross_near, saved_left)
            + product_flip(cross_far, saved_right)
        )
        coupling_rows = -cross_far
    coupling_rows = jnp.where(
        position == parts_count - 1, jnp.zeros_like(coupling_rows), coupling_rows
    )
    return (diagonal_rows[None], coupling_rows[None], pivot_rows[None])


def solution(mesh):
    placed = (
        P("tm", None, None),
        P("tm", None, "rows"),
        P("tm", "rows", None),
        P("tm", "rows", None),
    )
    return jax.shard_map(
        local,
        mesh=mesh,
        in_specs=placed,
        out_specs=(P("tm", "rows", None), P("tm", "rows", None), P("tm", "rows", None)),
        check_vma=False,
    )
```

```python
import jax
import jax.numpy as jnp
from jax import lax
from jax.sharding import PartitionSpec as P
from jax.experimental import pallas as pl
from jax.experimental.pallas import tpu as pltpu

LEVELS = 2
LEAF = 32
PIVOTS = 4


precise = lax.Precision.HIGHEST


def passed_along(value, axis, steps):
    count = lax.axis_size(axis)
    leading, last = (max(0, -steps), min(count, count - steps))
    return lax.ppermute(value, axis, [(source, source + steps) for source in range(leading, last)])


def product(left, right):
    return jnp.dot(left, right, precision=precise, preferred_element_type=jnp.float32)


def product_flip(left, right):
    return lax.dot_general(
        left, right, (((1,), (1,)), ((), ())), precision=precise, preferred_element_type=jnp.float32
    )


def product_over(left, right):
    return lax.dot_general(
        left, right, (((0,), (0,)), ((), ())), precision=precise, preferred_element_type=jnp.float32
    )


def strip_inverse(strip, offset):
    rows, width = strip.shape
    sub = lax.broadcasted_iota(jnp.int32, (rows, width), 0)
    lane = lax.broadcasted_iota(jnp.int32, (rows, width), 1)
    sub_col = lax.broadcasted_iota(jnp.int32, (rows, 1), 0)
    lane_row = lax.broadcasted_iota(jnp.int32, (1, width), 1)
    inside = (lane >= offset) & (lane < offset + rows)

    def step(group, held):
        k = PIVOTS * group
        row_masks = [sub == k + i for i in range(PIVOTS)]
        lane_masks = [lane == k + i + offset for i in range(PIVOTS)]
        rows_of = [jnp.sum(jnp.where(m, held, 0.0), axis=0, keepdims=True) for m in row_masks]
        cols_of = [jnp.sum(jnp.where(m, held, 0.0), axis=1, keepdims=True) for m in lane_masks]
        pivot = [
            [jnp.sum(jnp.where(sub_col == k + i, cols_of[j], 0.0), axis=0, keepdims=True) for j in range(PIVOTS)]
            for i in range(PIVOTS)
        ]
        for p in range(PIVOTS):
            inv_p = 1.0 / pivot[p][p]
            top = [pivot[p][j] * inv_p for j in range(PIVOTS)]
            top[p] = inv_p
            for i in range(PIVOTS):
                if i != p:
                    factor = pivot[i][p]
                    pivot[i] = [pivot[i][j] - factor * top[j] for j in range(PIVOTS)]
                    pivot[i][p] = -factor * inv_p
            pivot[p] = top
        lane_at = [lane_row == k + j + offset for j in range(PIVOTS)]
        for j in range(PIVOTS):
            value = rows_of[j]
            for m in range(PIVOTS):
                value = jnp.where(lane_at[m], 1.0 if m == j else 0.0, value)
            rows_of[j] = value
        new_rows = []
        for i in range(PIVOTS):
            total = pivot[i][0] * rows_of[0]
            for j in range(1, PIVOTS):
                total = total + pivot[i][j] * rows_of[j]
            new_rows.append(total)
        in_pivot = (sub_col >= k) & (sub_col < k + PIVOTS)
        any_lane = (lane >= k + offset) & (lane < k + offset + PIVOTS)
        held = jnp.where(any_lane, 0.0, held)
        for j in range(PIVOTS):
            held = held - jnp.where(in_pivot, 0.0, cols_of[j]) * new_rows[j]
        for i in range(PIVOTS):
            held = jnp.where(row_masks[i], new_rows[i], held)
        return held

    return lax.fori_loop(0, rows // PIVOTS, step, jnp.where(inside, strip, 0.0))


def eliminate(held, low, size, row_base, inverse_strip):
    rows, width = held.shape
    sub = lax.broadcasted_iota(jnp.int32, (rows, width), 0)
    lane = lax.broadcasted_iota(jnp.int32, (rows, width), 1)
    lanes_in = (lane >= low) & (lane < low + size)
    rows_in = (sub >= low) & (sub < low + size)
    span = held[row_base : row_base + 128, :]
    span_sub = sub[row_base : row_base + 128, :]
    span_lane = lane[row_base : row_base + 128, :]
    span_rows = jnp.where(
        (span_lane >= low) & (span_lane < low + size),
        (span_lane == span_sub).astype(jnp.float32),
        span,
    )
    row_new = jnp.dot(inverse_strip, span_rows, precision=precise, preferred_element_type=jnp.float32)
    pieces = []
    if low - row_base > 0:
        pieces.append(jnp.zeros((low - row_base, width), jnp.float32))
    pieces.append(row_new)
    if row_base + 128 - low - size > 0:
        pieces.append(jnp.zeros((row_base + 128 - low - size, width), jnp.float32))
    placed = jnp.concatenate(pieces, axis=0) if len(pieces) > 1 else row_new
    col_base = (low // 128) * 128
    cols = held[:, col_base : col_base + 128]
    cols = jnp.where(lanes_in[:, col_base : col_base + 128] & ~rows_in[:, col_base : col_base + 128], cols, 0.0)
    held = jnp.where(lanes_in, 0.0, held) - jnp.dot(cols, placed, precision=precise, preferred_element_type=jnp.float32)
    return jnp.where(rows_in, jnp.concatenate([jnp.zeros((row_base, width), jnp.float32), placed, jnp.zeros((rows - row_base - 128, width), jnp.float32)], axis=0) if rows > 128 else placed, held)


def block_inverse(block, leaf):
    for j in range(block.shape[0] // leaf):
        low = j * leaf
        inverse_strip = strip_inverse(block[low : low + leaf, :], low)
        block = eliminate(block, low, leaf, 0, inverse_strip)
    return block


def inverse_kernel(a_ref, o_ref):
    n = a_ref.shape[0]
    b = 128
    o_ref[...] = a_ref[...]
    sub_b = lax.broadcasted_iota(jnp.int32, (b, n), 0)
    lane_b = lax.broadcasted_iota(jnp.int32, (b, n), 1)
    sub_n = lax.broadcasted_iota(jnp.int32, (n, b), 0)
    lane_n = lax.broadcasted_iota(jnp.int32, (n, n), 1)
    for k in range(n // b):
        lo = k * b
        pivot_inv = block_inverse(o_ref[lo : lo + b, lo : lo + b], LEAF)
        in_block = (lane_b >= lo) & (lane_b < lo + b)
        row_block = jnp.where(in_block, (lane_b - lo == sub_b).astype(jnp.float32), o_ref[lo : lo + b, :])
        row_new = jnp.dot(pivot_inv, row_block, precision=precise, preferred_element_type=jnp.float32)
        col_block = o_ref[:, lo : lo + b]
        col_block = jnp.where((sub_n >= lo) & (sub_n < lo + b), 0.0, col_block)
        whole = jnp.where((lane_n >= lo) & (lane_n < lo + b), 0.0, o_ref[...])
        o_ref[...] = whole - jnp.dot(col_block, row_new, precision=precise, preferred_element_type=jnp.float32)
        o_ref[lo : lo + b, :] = row_new


def spd_inverse(matrix):
    n = matrix.shape[0]
    return pl.pallas_call(
        inverse_kernel,
        out_shape=jax.ShapeDtypeStruct((n, n), jnp.float32),
        in_specs=[pl.BlockSpec(memory_space=pltpu.VMEM)],
        out_specs=pl.BlockSpec(memory_space=pltpu.VMEM),
        cost_estimate=pl.CostEstimate(flops=2 * n * n * n, bytes_accessed=8 * n * n, transcendentals=0),
    )(matrix)


def local(pivot_blocks, lower_blocks, top_diagonal, top_coupling):
    parts_count = lax.axis_size("tm")
    position = lax.axis_index("tm")
    row_part = lax.axis_index("rows")
    full_width = pivot_blocks.shape[1]
    quarter = lower_blocks.shape[2]
    row_start = row_part * quarter
    first_pivot = pivot_blocks[0]
    lower_columns = jnp.where(position == 0, jnp.zeros_like(lower_blocks[0]), lower_blocks[0])
    next_columns = passed_along(lower_columns, "tm", -1)
    lower_whole = lax.all_gather(lower_columns, "rows", axis=1, tiled=True)
    upper_whole = lax.all_gather(next_columns, "rows", axis=1, tiled=True).T
    upper_columns = lax.dynamic_slice_in_dim(upper_whole, row_start, quarter, 1)
    pivot_rows = lax.dynamic_slice_in_dim(first_pivot, row_start, quarter, 0)
    saved = []
    for tier_index in range(LEVELS):
        spacing = 2**tier_index
        if tier_index == 0:
            whole_pivot = first_pivot
        else:
            whole_pivot = lax.all_gather(pivot_rows, "rows", axis=0, tiled=True)
            lower_whole = lax.all_gather(lower_columns, "rows", axis=1, tiled=True)
            upper_whole = lax.all_gather(upper_columns, "rows", axis=1, tiled=True)
        inverse_whole = spd_inverse(whole_pivot)
        inverse_columns = lax.dynamic_slice_in_dim(inverse_whole, row_start, quarter, 1)
        left_solved = product(inverse_whole, lower_whole)
        right_solved = product(inverse_whole, upper_whole)
        drop_left = product_over(lower_columns, left_solved)
        upper_new = -product_over(upper_columns, left_solved)
        left_bound = passed_along(jnp.stack([drop_left, upper_new]), "tm", -spacing)
        drop_right = product_over(upper_columns, right_solved)
        lower_new = -product_over(lower_columns, right_solved)
        right_bound = passed_along(jnp.stack([drop_right, lower_new]), "tm", spacing)
        pivot_rows = pivot_rows - left_bound[0] - right_bound[0]
        upper_columns = left_bound[1].T
        lower_columns = right_bound[1].T
        saved.append((left_solved, right_solved, inverse_columns))
    diagonal_rows = top_diagonal[0]
    coupling_rows = jnp.where(
        position + 2**LEVELS >= parts_count, jnp.zeros_like(top_coupling[0]), top_coupling[0]
    )
    for tier_index in reversed(range(LEVELS)):
        spacing = 2**tier_index
        saved_left, saved_right, saved_inverse = saved[tier_index]
        left_rows = lax.dynamic_slice_in_dim(saved_left, row_start, quarter, 0)
        right_rows = lax.dynamic_slice_in_dim(saved_right, row_start, quarter, 0)
        from_left = passed_along(jnp.stack([diagonal_rows, coupling_rows]), "tm", spacing)
        from_right = passed_along(diagonal_rows, "tm", -spacing)
        joined = lax.all_gather(
            jnp.concatenate([from_left, from_right[None]], 0), "rows", axis=1, tiled=True
        )
        near_diagonal = joined[0]
        near_next = joined[1]
        far_diagonal = joined[2]
        cross_near = product(left_rows, near_diagonal) + product_flip(right_rows, near_next)
        cross_far = product(left_rows, near_next) + product(right_rows, far_diagonal)
        diagonal_rows = (
            saved_inverse.T
            + product_flip(cross_near, saved_left)
            + product_flip(cross_far, saved_right)
        )
        coupling_rows = -cross_far
    coupling_rows = jnp.where(
        position == parts_count - 1, jnp.zeros_like(coupling_rows), coupling_rows
    )
    return (diagonal_rows[None], coupling_rows[None], pivot_rows[None])


def solution(mesh):
    placed = (
        P("tm", None, None),
        P("tm", None, "rows"),
        P("tm", "rows", None),
        P("tm", "rows", None),
    )
    return jax.shard_map(
        local,
        mesh=mesh,
        in_specs=placed,
        out_specs=(P("tm", "rows", None), P("tm", "rows", None), P("tm", "rows", None)),
        check_vma=False,
    )
```

```python
import jax
import jax.numpy as jnp
from jax import lax
from jax.sharding import PartitionSpec as P
from jax.experimental import pallas as pl
from jax.experimental.pallas import tpu as pltpu

LEVELS = 2
LEAF = 32
PIVOTS = 4


precise = lax.Precision.HIGHEST


def passed_along(value, axis, steps):
    count = lax.axis_size(axis)
    leading, last = (max(0, -steps), min(count, count - steps))
    return lax.ppermute(value, axis, [(source, source + steps) for source in range(leading, last)])


def product(left, right):
    return jnp.dot(left, right, precision=precise, preferred_element_type=jnp.float32)


def product_flip(left, right):
    return lax.dot_general(
        left, right, (((1,), (1,)), ((), ())), precision=precise, preferred_element_type=jnp.float32
    )


def product_over(left, right):
    return lax.dot_general(
        left, right, (((0,), (0,)), ((), ())), precision=precise, preferred_element_type=jnp.float32
    )


def strip_inverse(strip, offset):
    rows, width = strip.shape
    sub = lax.broadcasted_iota(jnp.int32, (rows, width), 0)
    lane = lax.broadcasted_iota(jnp.int32, (rows, width), 1)
    sub_col = lax.broadcasted_iota(jnp.int32, (rows, 1), 0)
    lane_row = lax.broadcasted_iota(jnp.int32, (1, width), 1)
    inside = (lane >= offset) & (lane < offset + rows)

    def step(group, held):
        k = PIVOTS * group
        row_masks = [sub == k + i for i in range(PIVOTS)]
        lane_masks = [lane == k + i + offset for i in range(PIVOTS)]
        rows_of = [jnp.sum(jnp.where(m, held, 0.0), axis=0, keepdims=True) for m in row_masks]
        cols_of = [jnp.sum(jnp.where(m, held, 0.0), axis=1, keepdims=True) for m in lane_masks]
        pivot = [
            [jnp.sum(jnp.where(sub_col == k + i, cols_of[j], 0.0), axis=0, keepdims=True) for j in range(PIVOTS)]
            for i in range(PIVOTS)
        ]
        for p in range(PIVOTS):
            inv_p = 1.0 / pivot[p][p]
            top = [pivot[p][j] * inv_p for j in range(PIVOTS)]
            top[p] = inv_p
            for i in range(PIVOTS):
                if i != p:
                    factor = pivot[i][p]
                    pivot[i] = [pivot[i][j] - factor * top[j] for j in range(PIVOTS)]
                    pivot[i][p] = -factor * inv_p
            pivot[p] = top
        lane_at = [lane_row == k + j + offset for j in range(PIVOTS)]
        for j in range(PIVOTS):
            value = rows_of[j]
            for m in range(PIVOTS):
                value = jnp.where(lane_at[m], 1.0 if m == j else 0.0, value)
            rows_of[j] = value
        new_rows = []
        for i in range(PIVOTS):
            total = pivot[i][0] * rows_of[0]
            for j in range(1, PIVOTS):
                total = total + pivot[i][j] * rows_of[j]
            new_rows.append(total)
        in_pivot = (sub_col >= k) & (sub_col < k + PIVOTS)
        any_lane = (lane >= k + offset) & (lane < k + offset + PIVOTS)
        held = jnp.where(any_lane, 0.0, held)
        for j in range(PIVOTS):
            held = held - jnp.where(in_pivot, 0.0, cols_of[j]) * new_rows[j]
        for i in range(PIVOTS):
            held = jnp.where(row_masks[i], new_rows[i], held)
        return held

    return lax.fori_loop(0, rows // PIVOTS, step, jnp.where(inside, strip, 0.0))


def eliminate(held, low, size, row_base, inverse_strip):
    rows, width = held.shape
    sub = lax.broadcasted_iota(jnp.int32, (rows, width), 0)
    lane = lax.broadcasted_iota(jnp.int32, (rows, width), 1)
    lanes_in = (lane >= low) & (lane < low + size)
    rows_in = (sub >= low) & (sub < low + size)
    span = held[row_base : row_base + 128, :]
    span_sub = sub[row_base : row_base + 128, :]
    span_lane = lane[row_base : row_base + 128, :]
    span_rows = jnp.where(
        (span_lane >= low) & (span_lane < low + size),
        (span_lane == span_sub).astype(jnp.float32),
        span,
    )
    row_new = jnp.dot(inverse_strip, span_rows, precision=precise, preferred_element_type=jnp.float32)
    pieces = []
    if low - row_base > 0:
        pieces.append(jnp.zeros((low - row_base, width), jnp.float32))
    pieces.append(row_new)
    if row_base + 128 - low - size > 0:
        pieces.append(jnp.zeros((row_base + 128 - low - size, width), jnp.float32))
    placed = jnp.concatenate(pieces, axis=0) if len(pieces) > 1 else row_new
    col_base = (low // 128) * 128
    cols = held[:, col_base : col_base + 128]
    cols = jnp.where(lanes_in[:, col_base : col_base + 128] & ~rows_in[:, col_base : col_base + 128], cols, 0.0)
    held = jnp.where(lanes_in, 0.0, held) - jnp.dot(cols, placed, precision=precise, preferred_element_type=jnp.float32)
    return jnp.where(rows_in, jnp.concatenate([jnp.zeros((row_base, width), jnp.float32), placed, jnp.zeros((rows - row_base - 128, width), jnp.float32)], axis=0) if rows > 128 else placed, held)


def block_inverse(block, leaf):
    for j in range(block.shape[0] // leaf):
        low = j * leaf
        inverse_strip = strip_inverse(block[low : low + leaf, :], low)
        block = eliminate(block, low, leaf, 0, inverse_strip)
    return block


def inverse_kernel(a_ref, o_ref):
    n = a_ref.shape[0]
    b = 128
    o_ref[...] = a_ref[...]
    sub_b = lax.broadcasted_iota(jnp.int32, (b, n), 0)
    lane_b = lax.broadcasted_iota(jnp.int32, (b, n), 1)
    sub_n = lax.broadcasted_iota(jnp.int32, (n, b), 0)
    lane_n = lax.broadcasted_iota(jnp.int32, (n, n), 1)
    for k in range(n // b):
        lo = k * b
        pivot_inv = block_inverse(o_ref[lo : lo + b, lo : lo + b], LEAF)
        in_block = (lane_b >= lo) & (lane_b < lo + b)
        row_block = jnp.where(in_block, (lane_b - lo == sub_b).astype(jnp.float32), o_ref[lo : lo + b, :])
        row_new = jnp.dot(pivot_inv, row_block, precision=precise, preferred_element_type=jnp.float32)
        col_block = o_ref[:, lo : lo + b]
        col_block = jnp.where((sub_n >= lo) & (sub_n < lo + b), 0.0, col_block)
        whole = jnp.where((lane_n >= lo) & (lane_n < lo + b), 0.0, o_ref[...])
        o_ref[...] = whole - jnp.dot(col_block, row_new, precision=precise, preferred_element_type=jnp.float32)
        o_ref[lo : lo + b, :] = row_new


def spd_inverse(matrix):
    n = matrix.shape[0]
    return pl.pallas_call(
        inverse_kernel,
        out_shape=jax.ShapeDtypeStruct((n, n), jnp.float32),
        in_specs=[pl.BlockSpec(memory_space=pltpu.VMEM)],
        out_specs=pl.BlockSpec(memory_space=pltpu.VMEM),
        cost_estimate=pl.CostEstimate(flops=2 * n * n * n, bytes_accessed=8 * n * n, transcendentals=0),
    )(matrix)


def local_body(pivot_blocks, lower_blocks, top_diagonal, top_coupling):
    parts_count = lax.axis_size("tm")
    position = lax.axis_index("tm")
    row_part = lax.axis_index("rows")
    quarter = lower_blocks.shape[2]
    row_start = row_part * quarter
    first_pivot = pivot_blocks[0]
    lower_columns = jnp.where(position == 0, jnp.zeros_like(lower_blocks[0]), lower_blocks[0])
    next_columns = passed_along(lower_columns, "tm", -1)
    lower_whole = lax.all_gather(lower_columns, "rows", axis=1, tiled=True)
    upper_whole = lax.all_gather(next_columns, "rows", axis=1, tiled=True).T
    upper_columns = lax.dynamic_slice_in_dim(upper_whole, row_start, quarter, 1)
    pivot_rows = lax.dynamic_slice_in_dim(first_pivot, row_start, quarter, 0)
    saved = []
    for tier_index in range(LEVELS):
        spacing = 2**tier_index
        if tier_index == 0:
            whole_pivot = first_pivot
        else:
            whole_pivot = lax.all_gather(pivot_rows, "rows", axis=0, tiled=True)
            lower_whole = lax.all_gather(lower_columns, "rows", axis=1, tiled=True)
            upper_whole = lax.all_gather(upper_columns, "rows", axis=1, tiled=True)
        inverse_whole = spd_inverse(whole_pivot)
        inverse_columns = lax.dynamic_slice_in_dim(inverse_whole, row_start, quarter, 1)
        left_solved = product(inverse_whole, lower_whole)
        right_solved = product(inverse_whole, upper_whole)
        drop_left = product_over(lower_columns, left_solved)
        upper_new = -product_over(upper_columns, left_solved)
        left_bound = passed_along(jnp.stack([drop_left, upper_new]), "tm", -spacing)
        drop_right = product_over(upper_columns, right_solved)
        lower_new = -product_over(lower_columns, right_solved)
        right_bound = passed_along(jnp.stack([drop_right, lower_new]), "tm", spacing)
        pivot_rows = pivot_rows - left_bound[0] - right_bound[0]
        upper_columns = left_bound[1].T
        lower_columns = right_bound[1].T
        saved.append((left_solved, right_solved, inverse_columns))
    diagonal_rows = top_diagonal[0]
    coupling_rows = jnp.where(
        position + 2**LEVELS >= parts_count, jnp.zeros_like(top_coupling[0]), top_coupling[0]
    )
    for tier_index in reversed(range(LEVELS)):
        spacing = 2**tier_index
        saved_left, saved_right, saved_inverse = saved[tier_index]
        left_rows = lax.dynamic_slice_in_dim(saved_left, row_start, quarter, 0)
        right_rows = lax.dynamic_slice_in_dim(saved_right, row_start, quarter, 0)
        from_left = passed_along(jnp.stack([diagonal_rows, coupling_rows]), "tm", spacing)
        from_right = passed_along(diagonal_rows, "tm", -spacing)
        joined = lax.all_gather(
            jnp.concatenate([from_left, from_right[None]], 0), "rows", axis=1, tiled=True
        )
        near_diagonal = joined[0]
        near_next = joined[1]
        far_diagonal = joined[2]
        cross_near = product(left_rows, near_diagonal) + product_flip(right_rows, near_next)
        cross_far = product(left_rows, near_next) + product(right_rows, far_diagonal)
        diagonal_rows = (
            saved_inverse.T
            + product_flip(cross_near, saved_left)
            + product_flip(cross_far, saved_right)
        )
        coupling_rows = -cross_far
    coupling_rows = jnp.where(
        position == parts_count - 1, jnp.zeros_like(coupling_rows), coupling_rows
    )
    return (diagonal_rows[None], coupling_rows[None], pivot_rows[None])


def solution(mesh):
    placed = (
        P("tm", None, None),
        P("tm", None, "rows"),
        P("tm", "rows", None),
        P("tm", "rows", None),
    )
    return jax.shard_map(
        local_body,
        mesh=mesh,
        in_specs=placed,
        out_specs=(P("tm", "rows", None), P("tm", "rows", None), P("tm", "rows", None)),
        check_vma=False,
    )
```

```python
import jax
import jax.numpy as jnp
from jax import lax
from jax.sharding import PartitionSpec as P
from jax.experimental import pallas as pl
from jax.experimental.pallas import tpu as pltpu

LEVELS = 2
LEAF = 32
PIVOTS = 4


precise = lax.Precision.HIGHEST


def passed_along(value, axis, steps):
    count = lax.axis_size(axis)
    leading, last = (max(0, -steps), min(count, count - steps))
    return lax.ppermute(value, axis, [(source, source + steps) for source in range(leading, last)])


def product(left, right):
    return jnp.dot(left, right, precision=precise, preferred_element_type=jnp.float32)


def product_flip(left, right):
    return lax.dot_general(
        left, right, (((1,), (1,)), ((), ())), precision=precise, preferred_element_type=jnp.float32
    )


def product_over(left, right):
    return lax.dot_general(
        left, right, (((0,), (0,)), ((), ())), precision=precise, preferred_element_type=jnp.float32
    )


def strip_inverse(strip, offset):
    rows, width = strip.shape
    sub = lax.broadcasted_iota(jnp.int32, (rows, width), 0)
    lane = lax.broadcasted_iota(jnp.int32, (rows, width), 1)
    sub_col = lax.broadcasted_iota(jnp.int32, (rows, 1), 0)
    lane_row = lax.broadcasted_iota(jnp.int32, (1, width), 1)
    inside = (lane >= offset) & (lane < offset + rows)

    def step(group, held):
        k = PIVOTS * group
        row_masks = [sub == k + i for i in range(PIVOTS)]
        lane_masks = [lane == k + i + offset for i in range(PIVOTS)]
        rows_of = [jnp.sum(jnp.where(m, held, 0.0), axis=0, keepdims=True) for m in row_masks]
        cols_of = [jnp.sum(jnp.where(m, held, 0.0), axis=1, keepdims=True) for m in lane_masks]
        pivot = [
            [jnp.sum(jnp.where(sub_col == k + i, cols_of[j], 0.0), axis=0, keepdims=True) for j in range(PIVOTS)]
            for i in range(PIVOTS)
        ]
        for p in range(PIVOTS):
            inv_p = 1.0 / pivot[p][p]
            top = [pivot[p][j] * inv_p for j in range(PIVOTS)]
            top[p] = inv_p
            for i in range(PIVOTS):
                if i != p:
                    factor = pivot[i][p]
                    pivot[i] = [pivot[i][j] - factor * top[j] for j in range(PIVOTS)]
                    pivot[i][p] = -factor * inv_p
            pivot[p] = top
        lane_at = [lane_row == k + j + offset for j in range(PIVOTS)]
        for j in range(PIVOTS):
            value = rows_of[j]
            for m in range(PIVOTS):
                value = jnp.where(lane_at[m], 1.0 if m == j else 0.0, value)
            rows_of[j] = value
        new_rows = []
        for i in range(PIVOTS):
            total = pivot[i][0] * rows_of[0]
            for j in range(1, PIVOTS):
                total = total + pivot[i][j] * rows_of[j]
            new_rows.append(total)
        in_pivot = (sub_col >= k) & (sub_col < k + PIVOTS)
        any_lane = (lane >= k + offset) & (lane < k + offset + PIVOTS)
        held = jnp.where(any_lane, 0.0, held)
        for j in range(PIVOTS):
            held = held - jnp.where(in_pivot, 0.0, cols_of[j]) * new_rows[j]
        for i in range(PIVOTS):
            held = jnp.where(row_masks[i], new_rows[i], held)
        return held

    return lax.fori_loop(0, rows // PIVOTS, step, jnp.where(inside, strip, 0.0))


def eliminate(held, low, size, row_base, inverse_strip):
    rows, width = held.shape
    sub = lax.broadcasted_iota(jnp.int32, (rows, width), 0)
    lane = lax.broadcasted_iota(jnp.int32, (rows, width), 1)
    lanes_in = (lane >= low) & (lane < low + size)
    rows_in = (sub >= low) & (sub < low + size)
    span = held[row_base : row_base + 128, :]
    span_sub = sub[row_base : row_base + 128, :]
    span_lane = lane[row_base : row_base + 128, :]
    span_rows = jnp.where(
        (span_lane >= low) & (span_lane < low + size),
        (span_lane == span_sub).astype(jnp.float32),
        span,
    )
    row_new = jnp.dot(inverse_strip, span_rows, precision=precise, preferred_element_type=jnp.float32)
    pieces = []
    if low - row_base > 0:
        pieces.append(jnp.zeros((low - row_base, width), jnp.float32))
    pieces.append(row_new)
    if row_base + 128 - low - size > 0:
        pieces.append(jnp.zeros((row_base + 128 - low - size, width), jnp.float32))
    placed = jnp.concatenate(pieces, axis=0) if len(pieces) > 1 else row_new
    col_base = (low // 128) * 128
    cols = held[:, col_base : col_base + 128]
    cols = jnp.where(lanes_in[:, col_base : col_base + 128] & ~rows_in[:, col_base : col_base + 128], cols, 0.0)
    held = jnp.where(lanes_in, 0.0, held) - jnp.dot(cols, placed, precision=precise, preferred_element_type=jnp.float32)
    return jnp.where(rows_in, jnp.concatenate([jnp.zeros((row_base, width), jnp.float32), placed, jnp.zeros((rows - row_base - 128, width), jnp.float32)], axis=0) if rows > 128 else placed, held)


def block_inverse(block, leaf):
    for j in range(block.shape[0] // leaf):
        low = j * leaf
        inverse_strip = strip_inverse(block[low : low + leaf, :], low)
        block = eliminate(block, low, leaf, 0, inverse_strip)
    return block


def inverse_kernel(a_ref, o_ref):
    n = a_ref.shape[0]
    b = 128
    o_ref[...] = a_ref[...]
    sub_b = lax.broadcasted_iota(jnp.int32, (b, n), 0)
    lane_b = lax.broadcasted_iota(jnp.int32, (b, n), 1)
    sub_n = lax.broadcasted_iota(jnp.int32, (n, b), 0)
    lane_n = lax.broadcasted_iota(jnp.int32, (n, n), 1)
    for k in range(n // b):
        lo = k * b
        pivot_inv = block_inverse(o_ref[lo : lo + b, lo : lo + b], LEAF)
        in_block = (lane_b >= lo) & (lane_b < lo + b)
        row_block = jnp.where(in_block, (lane_b - lo == sub_b).astype(jnp.float32), o_ref[lo : lo + b, :])
        row_new = jnp.dot(pivot_inv, row_block, precision=precise, preferred_element_type=jnp.float32)
        col_block = o_ref[:, lo : lo + b]
        col_block = jnp.where((sub_n >= lo) & (sub_n < lo + b), 0.0, col_block)
        whole = jnp.where((lane_n >= lo) & (lane_n < lo + b), 0.0, o_ref[...])
        o_ref[...] = whole - jnp.dot(col_block, row_new, precision=precise, preferred_element_type=jnp.float32)
        o_ref[lo : lo + b, :] = row_new


def spd_inverse(matrix):
    n = matrix.shape[0]
    return pl.pallas_call(
        inverse_kernel,
        out_shape=jax.ShapeDtypeStruct((n, n), jnp.float32),
        in_specs=[pl.BlockSpec(memory_space=pltpu.VMEM)],
        out_specs=pl.BlockSpec(memory_space=pltpu.VMEM),
        cost_estimate=pl.CostEstimate(flops=2 * n * n * n, bytes_accessed=8 * n * n, transcendentals=0),
    )(matrix)


def local_body(pivot_blocks, lower_blocks, top_diagonal, top_coupling):
    parts_count = lax.axis_size("tm")
    position = lax.axis_index("tm")
    row_part = lax.axis_index("rows")
    quarter = lower_blocks.shape[2]
    row_start = row_part * quarter
    first_pivot = pivot_blocks[0]
    lower_columns = jnp.where(position == 0, jnp.zeros_like(lower_blocks[0]), lower_blocks[0])
    next_columns = passed_along(lower_columns, "tm", -1)
    lower_whole = lax.all_gather(lower_columns, "rows", axis=1, tiled=True)
    upper_whole = lax.all_gather(next_columns, "rows", axis=1, tiled=True).T
    upper_columns = lax.dynamic_slice_in_dim(upper_whole, row_start, quarter, 1)
    pivot_rows = lax.dynamic_slice_in_dim(first_pivot, row_start, quarter, 0)
    saved = []
    for tier_index in range(LEVELS):
        spacing = 2**tier_index
        if tier_index == 0:
            whole_pivot = first_pivot
        else:
            whole_pivot = lax.all_gather(pivot_rows, "rows", axis=0, tiled=True)
            lower_whole = lax.all_gather(lower_columns, "rows", axis=1, tiled=True)
            upper_whole = lax.all_gather(upper_columns, "rows", axis=1, tiled=True)
        inverse_whole = spd_inverse(whole_pivot)
        inverse_columns = lax.dynamic_slice_in_dim(inverse_whole, row_start, quarter, 1)
        left_solved = product(inverse_whole, lower_whole)
        right_solved = product(inverse_whole, upper_whole)
        drop_left = product_over(lower_columns, left_solved)
        drop_right = product_over(upper_columns, right_solved)
        saved.append((left_solved, right_solved, inverse_columns))
        if tier_index == LEVELS - 1:
            left_drop = passed_along(drop_left, "tm", -spacing)
            right_drop = passed_along(drop_right, "tm", spacing)
            pivot_rows = pivot_rows - left_drop - right_drop
            break
        upper_new = -product_over(upper_columns, left_solved)
        left_bound = passed_along(jnp.stack([drop_left, upper_new]), "tm", -spacing)
        lower_new = -product_over(lower_columns, right_solved)
        right_bound = passed_along(jnp.stack([drop_right, lower_new]), "tm", spacing)
        pivot_rows = pivot_rows - left_bound[0] - right_bound[0]
        upper_columns = left_bound[1].T
        lower_columns = right_bound[1].T
    diagonal_rows = top_diagonal[0]
    coupling_rows = jnp.where(
        position + 2**LEVELS >= parts_count, jnp.zeros_like(top_coupling[0]), top_coupling[0]
    )
    for tier_index in reversed(range(LEVELS)):
        spacing = 2**tier_index
        saved_left, saved_right, saved_inverse = saved[tier_index]
        left_rows = lax.dynamic_slice_in_dim(saved_left, row_start, quarter, 0)
        right_rows = lax.dynamic_slice_in_dim(saved_right, row_start, quarter, 0)
        from_left = passed_along(jnp.stack([diagonal_rows, coupling_rows]), "tm", spacing)
        from_right = passed_along(diagonal_rows, "tm", -spacing)
        joined = lax.all_gather(
            jnp.concatenate([from_left, from_right[None]], 0), "rows", axis=1, tiled=True
        )
        near_diagonal = joined[0]
        near_next = joined[1]
        far_diagonal = joined[2]
        cross_near = product(left_rows, near_diagonal) + product_flip(right_rows, near_next)
        cross_far = product(left_rows, near_next) + product(right_rows, far_diagonal)
        diagonal_rows = saved_inverse.T + product_flip(cross_near, saved_left) + product_flip(cross_far, saved_right)
        coupling_rows = -cross_far
    coupling_rows = jnp.where(
        position == parts_count - 1, jnp.zeros_like(coupling_rows), coupling_rows
    )
    return (diagonal_rows[None], coupling_rows[None], pivot_rows[None])


def solution(mesh):
    placed = (
        P("tm", None, None),
        P("tm", None, "rows"),
        P("tm", "rows", None),
        P("tm", "rows", None),
    )
    return jax.shard_map(
        local_body,
        mesh=mesh,
        in_specs=placed,
        out_specs=(P("tm", "rows", None), P("tm", "rows", None), P("tm", "rows", None)),
        check_vma=False,
    )
```

```python
import functools

import jax
import jax.numpy as jnp
from jax import lax
from jax.sharding import PartitionSpec as P
from jax.experimental import pallas as pl
from jax.experimental.pallas import tpu as pltpu

LEVELS = 2
LEAF = 32
PIVOTS = 4


precise = lax.Precision.HIGHEST


def passed_along(value, axis, steps):
    count = lax.axis_size(axis)
    leading, last = (max(0, -steps), min(count, count - steps))
    return lax.ppermute(value, axis, [(source, source + steps) for source in range(leading, last)])


def product(left, right):
    return jnp.dot(left, right, precision=precise, preferred_element_type=jnp.float32)


def product_flip(left, right):
    return lax.dot_general(
        left, right, (((1,), (1,)), ((), ())), precision=precise, preferred_element_type=jnp.float32
    )


def product_over(left, right):
    return lax.dot_general(
        left, right, (((0,), (0,)), ((), ())), precision=precise, preferred_element_type=jnp.float32
    )


def strip_inverse(strip, offset):
    rows, width = strip.shape
    sub = lax.broadcasted_iota(jnp.int32, (rows, width), 0)
    lane = lax.broadcasted_iota(jnp.int32, (rows, width), 1)
    sub_col = lax.broadcasted_iota(jnp.int32, (rows, 1), 0)
    lane_row = lax.broadcasted_iota(jnp.int32, (1, width), 1)
    inside = (lane >= offset) & (lane < offset + rows)

    def step(group, held):
        k = PIVOTS * group
        row_masks = [sub == k + i for i in range(PIVOTS)]
        lane_masks = [lane == k + i + offset for i in range(PIVOTS)]
        rows_of = [jnp.sum(jnp.where(m, held, 0.0), axis=0, keepdims=True) for m in row_masks]
        cols_of = [jnp.sum(jnp.where(m, held, 0.0), axis=1, keepdims=True) for m in lane_masks]
        pivot = [
            [jnp.sum(jnp.where(sub_col == k + i, cols_of[j], 0.0), axis=0, keepdims=True) for j in range(PIVOTS)]
            for i in range(PIVOTS)
        ]
        for p in range(PIVOTS):
            inv_p = 1.0 / pivot[p][p]
            top = [pivot[p][j] * inv_p for j in range(PIVOTS)]
            top[p] = inv_p
            for i in range(PIVOTS):
                if i != p:
                    factor = pivot[i][p]
                    pivot[i] = [pivot[i][j] - factor * top[j] for j in range(PIVOTS)]
                    pivot[i][p] = -factor * inv_p
            pivot[p] = top
        lane_at = [lane_row == k + j + offset for j in range(PIVOTS)]
        for j in range(PIVOTS):
            value = rows_of[j]
            for m in range(PIVOTS):
                value = jnp.where(lane_at[m], 1.0 if m == j else 0.0, value)
            rows_of[j] = value
        new_rows = []
        for i in range(PIVOTS):
            total = pivot[i][0] * rows_of[0]
            for j in range(1, PIVOTS):
                total = total + pivot[i][j] * rows_of[j]
            new_rows.append(total)
        in_pivot = (sub_col >= k) & (sub_col < k + PIVOTS)
        any_lane = (lane >= k + offset) & (lane < k + offset + PIVOTS)
        held = jnp.where(any_lane, 0.0, held)
        for j in range(PIVOTS):
            held = held - jnp.where(in_pivot, 0.0, cols_of[j]) * new_rows[j]
        for i in range(PIVOTS):
            held = jnp.where(row_masks[i], new_rows[i], held)
        return held

    return lax.fori_loop(0, rows // PIVOTS, step, jnp.where(inside, strip, 0.0))


def eliminate(held, low, size, row_base, inverse_strip):
    rows, width = held.shape
    sub = lax.broadcasted_iota(jnp.int32, (rows, width), 0)
    lane = lax.broadcasted_iota(jnp.int32, (rows, width), 1)
    lanes_in = (lane >= low) & (lane < low + size)
    rows_in = (sub >= low) & (sub < low + size)
    span = held[row_base : row_base + 128, :]
    span_sub = sub[row_base : row_base + 128, :]
    span_lane = lane[row_base : row_base + 128, :]
    span_rows = jnp.where(
        (span_lane >= low) & (span_lane < low + size),
        (span_lane == span_sub).astype(jnp.float32),
        span,
    )
    row_new = jnp.dot(inverse_strip, span_rows, precision=precise, preferred_element_type=jnp.float32)
    pieces = []
    if low - row_base > 0:
        pieces.append(jnp.zeros((low - row_base, width), jnp.float32))
    pieces.append(row_new)
    if row_base + 128 - low - size > 0:
        pieces.append(jnp.zeros((row_base + 128 - low - size, width), jnp.float32))
    placed = jnp.concatenate(pieces, axis=0) if len(pieces) > 1 else row_new
    col_base = (low // 128) * 128
    cols = held[:, col_base : col_base + 128]
    cols = jnp.where(lanes_in[:, col_base : col_base + 128] & ~rows_in[:, col_base : col_base + 128], cols, 0.0)
    held = jnp.where(lanes_in, 0.0, held) - jnp.dot(cols, placed, precision=precise, preferred_element_type=jnp.float32)
    return jnp.where(rows_in, jnp.concatenate([jnp.zeros((row_base, width), jnp.float32), placed, jnp.zeros((rows - row_base - 128, width), jnp.float32)], axis=0) if rows > 128 else placed, held)


def block_inverse(block, leaf):
    for j in range(block.shape[0] // leaf):
        low = j * leaf
        inverse_strip = strip_inverse(block[low : low + leaf, :], low)
        block = eliminate(block, low, leaf, 0, inverse_strip)
    return block


def inverse_kernel(blocks, a_ref, o_ref):
    n = a_ref.shape[0]
    b = 128
    o_ref[...] = a_ref[...]
    sub_b = lax.broadcasted_iota(jnp.int32, (b, n), 0)
    lane_b = lax.broadcasted_iota(jnp.int32, (b, n), 1)
    sub_n = lax.broadcasted_iota(jnp.int32, (n, b), 0)
    lane_n = lax.broadcasted_iota(jnp.int32, (n, n), 1)
    for k in blocks:
        lo = k * b
        pivot_inv = block_inverse(o_ref[lo : lo + b, lo : lo + b], LEAF)
        in_block = (lane_b >= lo) & (lane_b < lo + b)
        row_block = jnp.where(in_block, (lane_b - lo == sub_b).astype(jnp.float32), o_ref[lo : lo + b, :])
        row_new = jnp.dot(pivot_inv, row_block, precision=precise, preferred_element_type=jnp.float32)
        col_block = o_ref[:, lo : lo + b]
        col_block = jnp.where((sub_n >= lo) & (sub_n < lo + b), 0.0, col_block)
        whole = jnp.where((lane_n >= lo) & (lane_n < lo + b), 0.0, o_ref[...])
        o_ref[...] = whole - jnp.dot(col_block, row_new, precision=precise, preferred_element_type=jnp.float32)
        o_ref[lo : lo + b, :] = row_new


def inverse_part(matrix, blocks):
    n = matrix.shape[0]
    return pl.pallas_call(
        functools.partial(inverse_kernel, blocks),
        out_shape=jax.ShapeDtypeStruct((n, n), jnp.float32),
        in_specs=[pl.BlockSpec(memory_space=pltpu.VMEM)],
        out_specs=pl.BlockSpec(memory_space=pltpu.VMEM),
        cost_estimate=pl.CostEstimate(flops=2 * n * n * n * len(blocks) // 4, bytes_accessed=8 * n * n, transcendentals=0),
    )(matrix)


def spd_inverse(matrix):
    count = matrix.shape[0] // 128
    half = count // 2
    partial_state = inverse_part(matrix, tuple(range(half)))
    return inverse_part(partial_state, tuple(range(half, count)))


def local_body(pivot_blocks, lower_blocks, top_diagonal, top_coupling):
    parts_count = lax.axis_size("tm")
    position = lax.axis_index("tm")
    row_part = lax.axis_index("rows")
    quarter = lower_blocks.shape[2]
    row_start = row_part * quarter
    first_pivot = pivot_blocks[0]
    lower_columns = jnp.where(position == 0, jnp.zeros_like(lower_blocks[0]), lower_blocks[0])
    next_columns = passed_along(lower_columns, "tm", -1)
    lower_whole = lax.all_gather(lower_columns, "rows", axis=1, tiled=True)
    upper_whole = lax.all_gather(next_columns, "rows", axis=1, tiled=True).T
    upper_columns = lax.dynamic_slice_in_dim(upper_whole, row_start, quarter, 1)
    pivot_rows = lax.dynamic_slice_in_dim(first_pivot, row_start, quarter, 0)
    saved = []
    for tier_index in range(LEVELS):
        spacing = 2**tier_index
        if tier_index == 0:
            whole_pivot = first_pivot
        else:
            whole_pivot = lax.all_gather(pivot_rows, "rows", axis=0, tiled=True)
            lower_whole = lax.all_gather(lower_columns, "rows", axis=1, tiled=True)
            upper_whole = lax.all_gather(upper_columns, "rows", axis=1, tiled=True)
        inverse_whole = spd_inverse(whole_pivot)
        inverse_columns = lax.dynamic_slice_in_dim(inverse_whole, row_start, quarter, 1)
        left_solved = product(inverse_whole, lower_whole)
        right_solved = product(inverse_whole, upper_whole)
        drop_left = product_over(lower_columns, left_solved)
        drop_right = product_over(upper_columns, right_solved)
        saved.append((left_solved, right_solved, inverse_columns))
        if tier_index == LEVELS - 1:
            left_drop = passed_along(drop_left, "tm", -spacing)
            right_drop = passed_along(drop_right, "tm", spacing)
            pivot_rows = pivot_rows - left_drop - right_drop
            break
        upper_new = -product_over(upper_columns, left_solved)
        left_bound = passed_along(jnp.stack([drop_left, upper_new]), "tm", -spacing)
        lower_new = -product_over(lower_columns, right_solved)
        right_bound = passed_along(jnp.stack([drop_right, lower_new]), "tm", spacing)
        pivot_rows = pivot_rows - left_bound[0] - right_bound[0]
        upper_columns = left_bound[1].T
        lower_columns = right_bound[1].T
    diagonal_rows = top_diagonal[0]
    coupling_rows = jnp.where(
        position + 2**LEVELS >= parts_count, jnp.zeros_like(top_coupling[0]), top_coupling[0]
    )
    for tier_index in reversed(range(LEVELS)):
        spacing = 2**tier_index
        saved_left, saved_right, saved_inverse = saved[tier_index]
        left_rows = lax.dynamic_slice_in_dim(saved_left, row_start, quarter, 0)
        right_rows = lax.dynamic_slice_in_dim(saved_right, row_start, quarter, 0)
        from_left = passed_along(jnp.stack([diagonal_rows, coupling_rows]), "tm", spacing)
        from_right = passed_along(diagonal_rows, "tm", -spacing)
        joined = lax.all_gather(
            jnp.concatenate([from_left, from_right[None]], 0), "rows", axis=1, tiled=True
        )
        near_diagonal = joined[0]
        near_next = joined[1]
        far_diagonal = joined[2]
        cross_near = product(left_rows, near_diagonal) + product_flip(right_rows, near_next)
        cross_far = product(left_rows, near_next) + product(right_rows, far_diagonal)
        diagonal_rows = saved_inverse.T + product_flip(cross_near, saved_left) + product_flip(cross_far, saved_right)
        coupling_rows = -cross_far
    coupling_rows = jnp.where(
        position == parts_count - 1, jnp.zeros_like(coupling_rows), coupling_rows
    )
    return (diagonal_rows[None], coupling_rows[None], pivot_rows[None])


def solution(mesh):
    placed = (
        P("tm", None, None),
        P("tm", None, "rows"),
        P("tm", "rows", None),
        P("tm", "rows", None),
    )
    return jax.shard_map(
        local_body,
        mesh=mesh,
        in_specs=placed,
        out_specs=(P("tm", "rows", None), P("tm", "rows", None), P("tm", "rows", None)),
        check_vma=False,
    )
```

```python
import functools

import jax
import jax.numpy as jnp
from jax import lax
from jax.sharding import PartitionSpec as P
from jax.experimental import pallas as pl
from jax.experimental.pallas import tpu as pltpu

LEVELS = 2
LEAF = 32
PIVOTS = 4


precise = lax.Precision.HIGHEST


def passed_along(value, axis, steps):
    count = lax.axis_size(axis)
    leading, last = (max(0, -steps), min(count, count - steps))
    return lax.ppermute(value, axis, [(source, source + steps) for source in range(leading, last)])


def product(left, right):
    return jnp.dot(left, right, precision=precise, preferred_element_type=jnp.float32)


def product_flip(left, right):
    return lax.dot_general(
        left, right, (((1,), (1,)), ((), ())), precision=precise, preferred_element_type=jnp.float32
    )


def product_over(left, right):
    return lax.dot_general(
        left, right, (((0,), (0,)), ((), ())), precision=precise, preferred_element_type=jnp.float32
    )


def strip_inverse(strip, offset):
    rows, width = strip.shape
    sub = lax.broadcasted_iota(jnp.int32, (rows, width), 0)
    lane = lax.broadcasted_iota(jnp.int32, (rows, width), 1)
    sub_col = lax.broadcasted_iota(jnp.int32, (rows, 1), 0)
    lane_row = lax.broadcasted_iota(jnp.int32, (1, width), 1)
    inside = (lane >= offset) & (lane < offset + rows)

    def step(group, held):
        k = PIVOTS * group
        row_masks = [sub == k + i for i in range(PIVOTS)]
        lane_masks = [lane == k + i + offset for i in range(PIVOTS)]
        rows_of = [jnp.sum(jnp.where(m, held, 0.0), axis=0, keepdims=True) for m in row_masks]
        cols_of = [jnp.sum(jnp.where(m, held, 0.0), axis=1, keepdims=True) for m in lane_masks]
        pivot = [
            [jnp.sum(jnp.where(sub_col == k + i, cols_of[j], 0.0), axis=0, keepdims=True) for j in range(PIVOTS)]
            for i in range(PIVOTS)
        ]
        for p in range(PIVOTS):
            inv_p = 1.0 / pivot[p][p]
            top = [pivot[p][j] * inv_p for j in range(PIVOTS)]
            top[p] = inv_p
            for i in range(PIVOTS):
                if i != p:
                    factor = pivot[i][p]
                    pivot[i] = [pivot[i][j] - factor * top[j] for j in range(PIVOTS)]
                    pivot[i][p] = -factor * inv_p
            pivot[p] = top
        lane_at = [lane_row == k + j + offset for j in range(PIVOTS)]
        for j in range(PIVOTS):
            value = rows_of[j]
            for m in range(PIVOTS):
                value = jnp.where(lane_at[m], 1.0 if m == j else 0.0, value)
            rows_of[j] = value
        new_rows = []
        for i in range(PIVOTS):
            total = pivot[i][0] * rows_of[0]
            for j in range(1, PIVOTS):
                total = total + pivot[i][j] * rows_of[j]
            new_rows.append(total)
        in_pivot = (sub_col >= k) & (sub_col < k + PIVOTS)
        any_lane = (lane >= k + offset) & (lane < k + offset + PIVOTS)
        held = jnp.where(any_lane, 0.0, held)
        for j in range(PIVOTS):
            held = held - jnp.where(in_pivot, 0.0, cols_of[j]) * new_rows[j]
        for i in range(PIVOTS):
            held = jnp.where(row_masks[i], new_rows[i], held)
        return held

    return lax.fori_loop(0, rows // PIVOTS, step, jnp.where(inside, strip, 0.0))


def eliminate(held, low, size, row_base, inverse_strip):
    rows, width = held.shape
    sub = lax.broadcasted_iota(jnp.int32, (rows, width), 0)
    lane = lax.broadcasted_iota(jnp.int32, (rows, width), 1)
    lanes_in = (lane >= low) & (lane < low + size)
    rows_in = (sub >= low) & (sub < low + size)
    span = held[row_base : row_base + 128, :]
    span_sub = sub[row_base : row_base + 128, :]
    span_lane = lane[row_base : row_base + 128, :]
    span_rows = jnp.where(
        (span_lane >= low) & (span_lane < low + size),
        (span_lane == span_sub).astype(jnp.float32),
        span,
    )
    row_new = jnp.dot(inverse_strip, span_rows, precision=precise, preferred_element_type=jnp.float32)
    pieces = []
    if low - row_base > 0:
        pieces.append(jnp.zeros((low - row_base, width), jnp.float32))
    pieces.append(row_new)
    if row_base + 128 - low - size > 0:
        pieces.append(jnp.zeros((row_base + 128 - low - size, width), jnp.float32))
    placed = jnp.concatenate(pieces, axis=0) if len(pieces) > 1 else row_new
    col_base = (low // 128) * 128
    cols = held[:, col_base : col_base + 128]
    cols = jnp.where(lanes_in[:, col_base : col_base + 128] & ~rows_in[:, col_base : col_base + 128], cols, 0.0)
    held = jnp.where(lanes_in, 0.0, held) - jnp.dot(cols, placed, precision=precise, preferred_element_type=jnp.float32)
    return jnp.where(rows_in, jnp.concatenate([jnp.zeros((row_base, width), jnp.float32), placed, jnp.zeros((rows - row_base - 128, width), jnp.float32)], axis=0) if rows > 128 else placed, held)


def block_inverse(block, leaf):
    for j in range(block.shape[0] // leaf):
        low = j * leaf
        inverse_strip = strip_inverse(block[low : low + leaf, :], low)
        block = eliminate(block, low, leaf, 0, inverse_strip)
    return block


def inverse_kernel(blocks, a_ref, o_ref):
    n = a_ref.shape[0]
    b = 128
    o_ref[...] = a_ref[...]
    sub_b = lax.broadcasted_iota(jnp.int32, (b, n), 0)
    lane_b = lax.broadcasted_iota(jnp.int32, (b, n), 1)
    sub_n = lax.broadcasted_iota(jnp.int32, (n, b), 0)
    lane_n = lax.broadcasted_iota(jnp.int32, (n, n), 1)
    for k in blocks:
        lo = k * b
        pivot_inv = block_inverse(o_ref[lo : lo + b, lo : lo + b], LEAF)
        in_block = (lane_b >= lo) & (lane_b < lo + b)
        row_block = jnp.where(in_block, (lane_b - lo == sub_b).astype(jnp.float32), o_ref[lo : lo + b, :])
        row_new = jnp.dot(pivot_inv, row_block, precision=precise, preferred_element_type=jnp.float32)
        col_block = o_ref[:, lo : lo + b]
        col_block = jnp.where((sub_n >= lo) & (sub_n < lo + b), 0.0, col_block)
        whole = jnp.where((lane_n >= lo) & (lane_n < lo + b), 0.0, o_ref[...])
        o_ref[...] = whole - jnp.dot(col_block, row_new, precision=precise, preferred_element_type=jnp.float32)
        o_ref[lo : lo + b, :] = row_new


def inverse_part(matrix, blocks):
    n = matrix.shape[0]
    return pl.pallas_call(
        functools.partial(inverse_kernel, blocks),
        out_shape=jax.ShapeDtypeStruct((n, n), jnp.float32),
        in_specs=[pl.BlockSpec(memory_space=pltpu.VMEM)],
        out_specs=pl.BlockSpec(memory_space=pltpu.VMEM),
        cost_estimate=pl.CostEstimate(flops=2 * n * n * n * len(blocks) // 4, bytes_accessed=8 * n * n, transcendentals=0),
    )(matrix)


def spd_inverse(matrix, split):
    count = matrix.shape[0] // 128
    if not split:
        return inverse_part(matrix, tuple(range(count)))
    half = count // 2
    partial_state = inverse_part(matrix, tuple(range(half)))
    return inverse_part(partial_state, tuple(range(half, count)))


def local_body(pivot_blocks, lower_blocks, top_diagonal, top_coupling):
    parts_count = lax.axis_size("tm")
    position = lax.axis_index("tm")
    row_part = lax.axis_index("rows")
    quarter = lower_blocks.shape[2]
    row_start = row_part * quarter
    first_pivot = pivot_blocks[0]
    lower_columns = jnp.where(position == 0, jnp.zeros_like(lower_blocks[0]), lower_blocks[0])
    next_columns = passed_along(lower_columns, "tm", -1)
    lower_whole = lax.all_gather(lower_columns, "rows", axis=1, tiled=True)
    upper_whole = lax.all_gather(next_columns, "rows", axis=1, tiled=True).T
    upper_columns = lax.dynamic_slice_in_dim(upper_whole, row_start, quarter, 1)
    pivot_rows = lax.dynamic_slice_in_dim(first_pivot, row_start, quarter, 0)
    saved = []
    for tier_index in range(LEVELS):
        spacing = 2**tier_index
        if tier_index == 0:
            whole_pivot = first_pivot
        else:
            whole_pivot = lax.all_gather(pivot_rows, "rows", axis=0, tiled=True)
            lower_whole = lax.all_gather(lower_columns, "rows", axis=1, tiled=True)
            upper_whole = lax.all_gather(upper_columns, "rows", axis=1, tiled=True)
        inverse_whole = spd_inverse(whole_pivot, tier_index == 0)
        inverse_columns = lax.dynamic_slice_in_dim(inverse_whole, row_start, quarter, 1)
        left_solved = product(inverse_whole, lower_whole)
        right_solved = product(inverse_whole, upper_whole)
        drop_left = product_over(lower_columns, left_solved)
        drop_right = product_over(upper_columns, right_solved)
        saved.append((left_solved, right_solved, inverse_columns))
        if tier_index == LEVELS - 1:
            left_drop = passed_along(drop_left, "tm", -spacing)
            right_drop = passed_along(drop_right, "tm", spacing)
            pivot_rows = pivot_rows - left_drop - right_drop
            break
        upper_new = -product_over(upper_columns, left_solved)
        left_bound = passed_along(jnp.stack([drop_left, upper_new]), "tm", -spacing)
        lower_new = -product_over(lower_columns, right_solved)
        right_bound = passed_along(jnp.stack([drop_right, lower_new]), "tm", spacing)
        pivot_rows = pivot_rows - left_bound[0] - right_bound[0]
        upper_columns = left_bound[1].T
        lower_columns = right_bound[1].T
    diagonal_rows = top_diagonal[0]
    coupling_rows = jnp.where(
        position + 2**LEVELS >= parts_count, jnp.zeros_like(top_coupling[0]), top_coupling[0]
    )
    for tier_index in reversed(range(LEVELS)):
        spacing = 2**tier_index
        saved_left, saved_right, saved_inverse = saved[tier_index]
        left_rows = lax.dynamic_slice_in_dim(saved_left, row_start, quarter, 0)
        right_rows = lax.dynamic_slice_in_dim(saved_right, row_start, quarter, 0)
        from_left = passed_along(jnp.stack([diagonal_rows, coupling_rows]), "tm", spacing)
        from_right = passed_along(diagonal_rows, "tm", -spacing)
        joined = lax.all_gather(
            jnp.concatenate([from_left, from_right[None]], 0), "rows", axis=1, tiled=True
        )
        near_diagonal = joined[0]
        near_next = joined[1]
        far_diagonal = joined[2]
        cross_near = product(left_rows, near_diagonal) + product_flip(right_rows, near_next)
        cross_far = product(left_rows, near_next) + product(right_rows, far_diagonal)
        diagonal_rows = saved_inverse.T + product_flip(cross_near, saved_left) + product_flip(cross_far, saved_right)
        coupling_rows = -cross_far
    coupling_rows = jnp.where(
        position == parts_count - 1, jnp.zeros_like(coupling_rows), coupling_rows
    )
    return (diagonal_rows[None], coupling_rows[None], pivot_rows[None])


def solution(mesh):
    placed = (
        P("tm", None, None),
        P("tm", None, "rows"),
        P("tm", "rows", None),
        P("tm", "rows", None),
    )
    return jax.shard_map(
        local_body,
        mesh=mesh,
        in_specs=placed,
        out_specs=(P("tm", "rows", None), P("tm", "rows", None), P("tm", "rows", None)),
        check_vma=False,
    )
```

```python
import functools

import jax
import jax.numpy as jnp
from jax import lax
from jax.sharding import PartitionSpec as P
from jax.experimental import pallas as pl
from jax.experimental.pallas import tpu as pltpu

LEVELS = 2
LEAF = 32
PIVOTS = 4


precise = lax.Precision.HIGHEST


def passed_along(value, axis, steps):
    count = lax.axis_size(axis)
    leading, last = (max(0, -steps), min(count, count - steps))
    return lax.ppermute(value, axis, [(source, source + steps) for source in range(leading, last)])


def product(left, right):
    return jnp.dot(left, right, precision=precise, preferred_element_type=jnp.float32)


def product_flip(left, right):
    return lax.dot_general(
        left, right, (((1,), (1,)), ((), ())), precision=precise, preferred_element_type=jnp.float32
    )


def product_over(left, right):
    return lax.dot_general(
        left, right, (((0,), (0,)), ((), ())), precision=precise, preferred_element_type=jnp.float32
    )


def strip_inverse(strip, offset):
    rows, width = strip.shape
    sub = lax.broadcasted_iota(jnp.int32, (rows, width), 0)
    lane = lax.broadcasted_iota(jnp.int32, (rows, width), 1)
    sub_col = lax.broadcasted_iota(jnp.int32, (rows, 1), 0)
    lane_row = lax.broadcasted_iota(jnp.int32, (1, width), 1)
    inside = (lane >= offset) & (lane < offset + rows)

    def step(group, held):
        k = PIVOTS * group
        row_masks = [sub == k + i for i in range(PIVOTS)]
        lane_masks = [lane == k + i + offset for i in range(PIVOTS)]
        rows_of = [jnp.sum(jnp.where(m, held, 0.0), axis=0, keepdims=True) for m in row_masks]
        cols_of = [jnp.sum(jnp.where(m, held, 0.0), axis=1, keepdims=True) for m in lane_masks]
        pivot = [
            [jnp.sum(jnp.where(sub_col == k + i, cols_of[j], 0.0), axis=0, keepdims=True) for j in range(PIVOTS)]
            for i in range(PIVOTS)
        ]
        for p in range(PIVOTS):
            inv_p = 1.0 / pivot[p][p]
            top = [pivot[p][j] * inv_p for j in range(PIVOTS)]
            top[p] = inv_p
            for i in range(PIVOTS):
                if i != p:
                    factor = pivot[i][p]
                    pivot[i] = [pivot[i][j] - factor * top[j] for j in range(PIVOTS)]
                    pivot[i][p] = -factor * inv_p
            pivot[p] = top
        lane_at = [lane_row == k + j + offset for j in range(PIVOTS)]
        for j in range(PIVOTS):
            value = rows_of[j]
            for m in range(PIVOTS):
                value = jnp.where(lane_at[m], 1.0 if m == j else 0.0, value)
            rows_of[j] = value
        new_rows = []
        for i in range(PIVOTS):
            total = pivot[i][0] * rows_of[0]
            for j in range(1, PIVOTS):
                total = total + pivot[i][j] * rows_of[j]
            new_rows.append(total)
        in_pivot = (sub_col >= k) & (sub_col < k + PIVOTS)
        any_lane = (lane >= k + offset) & (lane < k + offset + PIVOTS)
        held = jnp.where(any_lane, 0.0, held)
        for j in range(PIVOTS):
            held = held - jnp.where(in_pivot, 0.0, cols_of[j]) * new_rows[j]
        for i in range(PIVOTS):
            held = jnp.where(row_masks[i], new_rows[i], held)
        return held

    return lax.fori_loop(0, rows // PIVOTS, step, jnp.where(inside, strip, 0.0))


def eliminate(held, low, size, row_base, inverse_strip):
    rows, width = held.shape
    sub = lax.broadcasted_iota(jnp.int32, (rows, width), 0)
    lane = lax.broadcasted_iota(jnp.int32, (rows, width), 1)
    lanes_in = (lane >= low) & (lane < low + size)
    rows_in = (sub >= low) & (sub < low + size)
    span = held[row_base : row_base + 128, :]
    span_sub = sub[row_base : row_base + 128, :]
    span_lane = lane[row_base : row_base + 128, :]
    span_rows = jnp.where(
        (span_lane >= low) & (span_lane < low + size),
        (span_lane == span_sub).astype(jnp.float32),
        span,
    )
    row_new = jnp.dot(inverse_strip, span_rows, precision=precise, preferred_element_type=jnp.float32)
    pieces = []
    if low - row_base > 0:
        pieces.append(jnp.zeros((low - row_base, width), jnp.float32))
    pieces.append(row_new)
    if row_base + 128 - low - size > 0:
        pieces.append(jnp.zeros((row_base + 128 - low - size, width), jnp.float32))
    placed = jnp.concatenate(pieces, axis=0) if len(pieces) > 1 else row_new
    col_base = (low // 128) * 128
    cols = held[:, col_base : col_base + 128]
    cols = jnp.where(lanes_in[:, col_base : col_base + 128] & ~rows_in[:, col_base : col_base + 128], cols, 0.0)
    held = jnp.where(lanes_in, 0.0, held) - jnp.dot(cols, placed, precision=precise, preferred_element_type=jnp.float32)
    return jnp.where(rows_in, jnp.concatenate([jnp.zeros((row_base, width), jnp.float32), placed, jnp.zeros((rows - row_base - 128, width), jnp.float32)], axis=0) if rows > 128 else placed, held)


def block_inverse(block, leaf):
    for j in range(block.shape[0] // leaf):
        low = j * leaf
        inverse_strip = strip_inverse(block[low : low + leaf, :], low)
        block = eliminate(block, low, leaf, 0, inverse_strip)
    return block


def inverse_kernel(blocks, a_ref, o_ref):
    n = a_ref.shape[0]
    b = 128
    o_ref[...] = a_ref[...]
    sub_b = lax.broadcasted_iota(jnp.int32, (b, n), 0)
    lane_b = lax.broadcasted_iota(jnp.int32, (b, n), 1)
    sub_n = lax.broadcasted_iota(jnp.int32, (n, b), 0)
    lane_n = lax.broadcasted_iota(jnp.int32, (n, n), 1)
    for k in blocks:
        lo = k * b
        pivot_inv = block_inverse(o_ref[lo : lo + b, lo : lo + b], LEAF)
        in_block = (lane_b >= lo) & (lane_b < lo + b)
        row_block = jnp.where(in_block, (lane_b - lo == sub_b).astype(jnp.float32), o_ref[lo : lo + b, :])
        row_new = jnp.dot(pivot_inv, row_block, precision=precise, preferred_element_type=jnp.float32)
        col_block = o_ref[:, lo : lo + b]
        col_block = jnp.where((sub_n >= lo) & (sub_n < lo + b), 0.0, col_block)
        whole = jnp.where((lane_n >= lo) & (lane_n < lo + b), 0.0, o_ref[...])
        o_ref[...] = whole - jnp.dot(col_block, row_new, precision=precise, preferred_element_type=jnp.float32)
        o_ref[lo : lo + b, :] = row_new


def inverse_part(matrix, blocks):
    n = matrix.shape[0]
    return pl.pallas_call(
        functools.partial(inverse_kernel, blocks),
        out_shape=jax.ShapeDtypeStruct((n, n), jnp.float32),
        in_specs=[pl.BlockSpec(memory_space=pltpu.VMEM)],
        out_specs=pl.BlockSpec(memory_space=pltpu.VMEM),
        cost_estimate=pl.CostEstimate(flops=2 * n * n * n * len(blocks) // 4, bytes_accessed=8 * n * n, transcendentals=0),
    )(matrix)


def spd_inverse(matrix, split):
    count = matrix.shape[0] // 128
    if not split:
        return inverse_part(matrix, tuple(range(count)))
    half = count // 2
    partial_state = inverse_part(matrix, tuple(range(half)))
    return inverse_part(partial_state, tuple(range(half, count)))


def local_body(pivot_blocks, lower_blocks, top_diagonal, top_coupling):
    parts_count = lax.axis_size("tm")
    position = lax.axis_index("tm")
    row_part = lax.axis_index("rows")
    quarter = lower_blocks.shape[2]
    row_start = row_part * quarter
    first_pivot = pivot_blocks[0]
    lower_columns = jnp.where(position == 0, jnp.zeros_like(lower_blocks[0]), lower_blocks[0])
    next_columns = passed_along(lower_columns, "tm", -1)
    lower_whole = lax.all_gather(lower_columns, "rows", axis=1, tiled=True)
    upper_whole = lax.all_gather(next_columns, "rows", axis=1, tiled=True).T
    upper_columns = lax.dynamic_slice_in_dim(upper_whole, row_start, quarter, 1)
    pivot_rows = lax.dynamic_slice_in_dim(first_pivot, row_start, quarter, 0)
    saved = []
    for tier_index in range(LEVELS):
        spacing = 2**tier_index
        if tier_index == 0:
            whole_pivot = first_pivot
        else:
            whole_pivot = lax.all_gather(pivot_rows, "rows", axis=0, tiled=True)
            lower_whole = lax.all_gather(lower_columns, "rows", axis=1, tiled=True)
            upper_whole = lax.all_gather(upper_columns, "rows", axis=1, tiled=True)
        inverse_whole = spd_inverse(whole_pivot, tier_index == 0)
        inverse_columns = lax.dynamic_slice_in_dim(inverse_whole, row_start, quarter, 1)
        left_solved = product(inverse_whole, lower_whole)
        right_solved = product(inverse_whole, upper_whole)
        drop_left = product_over(lower_columns, left_solved)
        drop_right = product_over(upper_columns, right_solved)
        saved.append((left_solved, right_solved, inverse_columns))
        if tier_index == LEVELS - 1:
            left_drop = passed_along(drop_left, "tm", -spacing)
            right_drop = passed_along(drop_right, "tm", spacing)
            pivot_rows = pivot_rows - left_drop - right_drop
            break
        upper_new = -product_over(upper_columns, left_solved)
        left_bound = passed_along(jnp.stack([drop_left, upper_new]), "tm", -spacing)
        lower_new = -product_over(lower_columns, right_solved)
        right_bound = passed_along(jnp.stack([drop_right, lower_new]), "tm", spacing)
        pivot_rows = pivot_rows - left_bound[0] - right_bound[0]
        upper_columns = left_bound[1].T
        lower_columns = right_bound[1].T
    diagonal_rows = top_diagonal[0]
    coupling_rows = jnp.where(
        position + 2**LEVELS >= parts_count, jnp.zeros_like(top_coupling[0]), top_coupling[0]
    )
    for tier_index in reversed(range(LEVELS)):
        spacing = 2**tier_index
        saved_left, saved_right, saved_inverse = saved[tier_index]
        left_rows = lax.dynamic_slice_in_dim(saved_left, row_start, quarter, 0)
        right_rows = lax.dynamic_slice_in_dim(saved_right, row_start, quarter, 0)
        from_left = passed_along(jnp.stack([diagonal_rows, coupling_rows]), "tm", spacing)
        from_right = passed_along(diagonal_rows, "tm", -spacing)
        joined = lax.all_gather(from_left, "rows", axis=1, tiled=True)
        far_diagonal = lax.all_gather(from_right, "rows", axis=0, tiled=True)
        near_diagonal = joined[0]
        near_next = joined[1]
        cross_near = product(left_rows, near_diagonal) + product_flip(right_rows, near_next)
        cross_far = product(left_rows, near_next) + product(right_rows, far_diagonal)
        diagonal_rows = saved_inverse.T + product_flip(cross_near, saved_left) + product_flip(cross_far, saved_right)
        coupling_rows = -cross_far
    coupling_rows = jnp.where(
        position == parts_count - 1, jnp.zeros_like(coupling_rows), coupling_rows
    )
    return (diagonal_rows[None], coupling_rows[None], pivot_rows[None])


def solution(mesh):
    placed = (
        P("tm", None, None),
        P("tm", None, "rows"),
        P("tm", "rows", None),
        P("tm", "rows", None),
    )
    return jax.shard_map(
        local_body,
        mesh=mesh,
        in_specs=placed,
        out_specs=(P("tm", "rows", None), P("tm", "rows", None), P("tm", "rows", None)),
        check_vma=False,
    )
```

```python
import functools

import jax
import jax.numpy as jnp
from jax import lax
from jax.sharding import PartitionSpec as P
from jax.experimental import pallas as pl
from jax.experimental.pallas import tpu as pltpu

LEVELS = 2
LEAF = 32
PIVOTS = 4


precise = lax.Precision.HIGHEST


def passed_along(value, axis, steps):
    count = lax.axis_size(axis)
    leading, last = (max(0, -steps), min(count, count - steps))
    return lax.ppermute(value, axis, [(source, source + steps) for source in range(leading, last)])


def shift_coupling(coupling_rows, spacing):
    return passed_along(coupling_rows, "tm", spacing)


def product(left, right):
    return jnp.dot(left, right, precision=precise, preferred_element_type=jnp.float32)


def product_flip(left, right):
    return lax.dot_general(
        left, right, (((1,), (1,)), ((), ())), precision=precise, preferred_element_type=jnp.float32
    )


def product_over(left, right):
    return lax.dot_general(
        left, right, (((0,), (0,)), ((), ())), precision=precise, preferred_element_type=jnp.float32
    )


def strip_inverse(strip, offset):
    rows, width = strip.shape
    sub = lax.broadcasted_iota(jnp.int32, (rows, width), 0)
    lane = lax.broadcasted_iota(jnp.int32, (rows, width), 1)
    sub_col = lax.broadcasted_iota(jnp.int32, (rows, 1), 0)
    lane_row = lax.broadcasted_iota(jnp.int32, (1, width), 1)
    inside = (lane >= offset) & (lane < offset + rows)

    def step(group, held):
        k = PIVOTS * group
        row_masks = [sub == k + i for i in range(PIVOTS)]
        lane_masks = [lane == k + i + offset for i in range(PIVOTS)]
        rows_of = [jnp.sum(jnp.where(m, held, 0.0), axis=0, keepdims=True) for m in row_masks]
        cols_of = [jnp.sum(jnp.where(m, held, 0.0), axis=1, keepdims=True) for m in lane_masks]
        pivot = [
            [jnp.sum(jnp.where(sub_col == k + i, cols_of[j], 0.0), axis=0, keepdims=True) for j in range(PIVOTS)]
            for i in range(PIVOTS)
        ]
        for p in range(PIVOTS):
            inv_p = 1.0 / pivot[p][p]
            top = [pivot[p][j] * inv_p for j in range(PIVOTS)]
            top[p] = inv_p
            for i in range(PIVOTS):
                if i != p:
                    factor = pivot[i][p]
                    pivot[i] = [pivot[i][j] - factor * top[j] for j in range(PIVOTS)]
                    pivot[i][p] = -factor * inv_p
            pivot[p] = top
        lane_at = [lane_row == k + j + offset for j in range(PIVOTS)]
        for j in range(PIVOTS):
            value = rows_of[j]
            for m in range(PIVOTS):
                value = jnp.where(lane_at[m], 1.0 if m == j else 0.0, value)
            rows_of[j] = value
        new_rows = []
        for i in range(PIVOTS):
            total = pivot[i][0] * rows_of[0]
            for j in range(1, PIVOTS):
                total = total + pivot[i][j] * rows_of[j]
            new_rows.append(total)
        in_pivot = (sub_col >= k) & (sub_col < k + PIVOTS)
        any_lane = (lane >= k + offset) & (lane < k + offset + PIVOTS)
        held = jnp.where(any_lane, 0.0, held)
        for j in range(PIVOTS):
            held = held - jnp.where(in_pivot, 0.0, cols_of[j]) * new_rows[j]
        for i in range(PIVOTS):
            held = jnp.where(row_masks[i], new_rows[i], held)
        return held

    return lax.fori_loop(0, rows // PIVOTS, step, jnp.where(inside, strip, 0.0))


def eliminate(held, low, size, row_base, inverse_strip):
    rows, width = held.shape
    sub = lax.broadcasted_iota(jnp.int32, (rows, width), 0)
    lane = lax.broadcasted_iota(jnp.int32, (rows, width), 1)
    lanes_in = (lane >= low) & (lane < low + size)
    rows_in = (sub >= low) & (sub < low + size)
    span = held[row_base : row_base + 128, :]
    span_sub = sub[row_base : row_base + 128, :]
    span_lane = lane[row_base : row_base + 128, :]
    span_rows = jnp.where(
        (span_lane >= low) & (span_lane < low + size),
        (span_lane == span_sub).astype(jnp.float32),
        span,
    )
    row_new = jnp.dot(inverse_strip, span_rows, precision=precise, preferred_element_type=jnp.float32)
    pieces = []
    if low - row_base > 0:
        pieces.append(jnp.zeros((low - row_base, width), jnp.float32))
    pieces.append(row_new)
    if row_base + 128 - low - size > 0:
        pieces.append(jnp.zeros((row_base + 128 - low - size, width), jnp.float32))
    placed = jnp.concatenate(pieces, axis=0) if len(pieces) > 1 else row_new
    col_base = (low // 128) * 128
    cols = held[:, col_base : col_base + 128]
    cols = jnp.where(lanes_in[:, col_base : col_base + 128] & ~rows_in[:, col_base : col_base + 128], cols, 0.0)
    held = jnp.where(lanes_in, 0.0, held) - jnp.dot(cols, placed, precision=precise, preferred_element_type=jnp.float32)
    return jnp.where(rows_in, jnp.concatenate([jnp.zeros((row_base, width), jnp.float32), placed, jnp.zeros((rows - row_base - 128, width), jnp.float32)], axis=0) if rows > 128 else placed, held)


def block_inverse(block, leaf):
    for j in range(block.shape[0] // leaf):
        low = j * leaf
        inverse_strip = strip_inverse(block[low : low + leaf, :], low)
        block = eliminate(block, low, leaf, 0, inverse_strip)
    return block


def inverse_kernel(blocks, a_ref, o_ref):
    n = a_ref.shape[0]
    b = 128
    o_ref[...] = a_ref[...]
    sub_b = lax.broadcasted_iota(jnp.int32, (b, n), 0)
    lane_b = lax.broadcasted_iota(jnp.int32, (b, n), 1)
    sub_n = lax.broadcasted_iota(jnp.int32, (n, b), 0)
    lane_n = lax.broadcasted_iota(jnp.int32, (n, n), 1)
    for k in blocks:
        lo = k * b
        pivot_inv = block_inverse(o_ref[lo : lo + b, lo : lo + b], LEAF)
        in_block = (lane_b >= lo) & (lane_b < lo + b)
        row_block = jnp.where(in_block, (lane_b - lo == sub_b).astype(jnp.float32), o_ref[lo : lo + b, :])
        row_new = jnp.dot(pivot_inv, row_block, precision=precise, preferred_element_type=jnp.float32)
        col_block = o_ref[:, lo : lo + b]
        col_block = jnp.where((sub_n >= lo) & (sub_n < lo + b), 0.0, col_block)
        whole = jnp.where((lane_n >= lo) & (lane_n < lo + b), 0.0, o_ref[...])
        o_ref[...] = whole - jnp.dot(col_block, row_new, precision=precise, preferred_element_type=jnp.float32)
        o_ref[lo : lo + b, :] = row_new


def inverse_part(matrix, blocks):
    n = matrix.shape[0]
    return pl.pallas_call(
        functools.partial(inverse_kernel, blocks),
        out_shape=jax.ShapeDtypeStruct((n, n), jnp.float32),
        in_specs=[pl.BlockSpec(memory_space=pltpu.VMEM)],
        out_specs=pl.BlockSpec(memory_space=pltpu.VMEM),
        cost_estimate=pl.CostEstimate(flops=2 * n * n * n * len(blocks) // 4, bytes_accessed=8 * n * n, transcendentals=0),
    )(matrix)


def spd_inverse(matrix, split):
    count = matrix.shape[0] // 128
    if not split:
        return inverse_part(matrix, tuple(range(count)))
    half = count // 2
    partial_state = inverse_part(matrix, tuple(range(half)))
    return inverse_part(partial_state, tuple(range(half, count)))


def local_body(pivot_blocks, lower_blocks, top_diagonal, top_coupling):
    parts_count = lax.axis_size("tm")
    position = lax.axis_index("tm")
    row_part = lax.axis_index("rows")
    quarter = lower_blocks.shape[2]
    row_start = row_part * quarter
    first_pivot = pivot_blocks[0]
    lower_columns = jnp.where(position == 0, jnp.zeros_like(lower_blocks[0]), lower_blocks[0])
    next_columns = passed_along(lower_columns, "tm", -1)
    lower_whole = lax.all_gather(lower_columns, "rows", axis=1, tiled=True)
    upper_whole = lax.all_gather(next_columns, "rows", axis=1, tiled=True).T
    upper_columns = lax.dynamic_slice_in_dim(upper_whole, row_start, quarter, 1)
    pivot_rows = lax.dynamic_slice_in_dim(first_pivot, row_start, quarter, 0)
    saved = []
    for tier_index in range(LEVELS):
        spacing = 2**tier_index
        if tier_index == 0:
            whole_pivot = first_pivot
        else:
            whole_pivot = lax.all_gather(pivot_rows, "rows", axis=0, tiled=True)
            lower_whole = lax.all_gather(lower_columns, "rows", axis=1, tiled=True)
            upper_whole = lax.all_gather(upper_columns, "rows", axis=1, tiled=True)
        inverse_whole = spd_inverse(whole_pivot, tier_index == 0)
        inverse_columns = lax.dynamic_slice_in_dim(inverse_whole, row_start, quarter, 1)
        left_solved = product(inverse_whole, lower_whole)
        right_solved = product(inverse_whole, upper_whole)
        drop_left = product_over(lower_columns, left_solved)
        drop_right = product_over(upper_columns, right_solved)
        saved.append((left_solved, right_solved, inverse_columns))
        if tier_index == LEVELS - 1:
            left_drop = passed_along(drop_left, "tm", -spacing)
            right_drop = passed_along(drop_right, "tm", spacing)
            pivot_rows = pivot_rows - left_drop - right_drop
            break
        upper_new = -product_over(upper_columns, left_solved)
        left_bound = passed_along(jnp.stack([drop_left, upper_new]), "tm", -spacing)
        lower_new = -product_over(lower_columns, right_solved)
        right_bound = passed_along(jnp.stack([drop_right, lower_new]), "tm", spacing)
        pivot_rows = pivot_rows - left_bound[0] - right_bound[0]
        upper_columns = left_bound[1].T
        lower_columns = right_bound[1].T
    diagonal_rows = top_diagonal[0]
    coupling_rows = jnp.where(
        position + 2**LEVELS >= parts_count, jnp.zeros_like(top_coupling[0]), top_coupling[0]
    )
    for tier_index in reversed(range(LEVELS)):
        spacing = 2**tier_index
        saved_left, saved_right, saved_inverse = saved[tier_index]
        left_rows = lax.dynamic_slice_in_dim(saved_left, row_start, quarter, 0)
        right_rows = lax.dynamic_slice_in_dim(saved_right, row_start, quarter, 0)
        from_left = jnp.stack(
            [passed_along(diagonal_rows, "tm", spacing), shift_coupling(coupling_rows, spacing)]
        )
        from_right = passed_along(diagonal_rows, "tm", -spacing)
        joined = lax.all_gather(
            jnp.concatenate([from_left, from_right[None]], 0), "rows", axis=1, tiled=True
        )
        near_diagonal = joined[0]
        near_next = joined[1]
        far_diagonal = joined[2]
        cross_near = product(left_rows, near_diagonal) + product_flip(right_rows, near_next)
        cross_far = product(left_rows, near_next) + product(right_rows, far_diagonal)
        diagonal_rows = saved_inverse.T + product_flip(cross_near, saved_left) + product_flip(cross_far, saved_right)
        coupling_rows = -cross_far
    coupling_rows = jnp.where(
        position == parts_count - 1, jnp.zeros_like(coupling_rows), coupling_rows
    )
    return (diagonal_rows[None], coupling_rows[None], pivot_rows[None])


def solution(mesh):
    placed = (
        P("tm", None, None),
        P("tm", None, "rows"),
        P("tm", "rows", None),
        P("tm", "rows", None),
    )
    return jax.shard_map(
        local_body,
        mesh=mesh,
        in_specs=placed,
        out_specs=(P("tm", "rows", None), P("tm", "rows", None), P("tm", "rows", None)),
        check_vma=False,
    )
```
